128 devices in a mesh: sec: 4 (over z), blk: 32 (over x, y, core).
Axes of the slice: x: 4, y: 4, z: 4, core: 2. Of those that a mesh axis runs over, the one named last changes fastest.
Arguments:
- fluid_state: float32 [5, 128, 512, 256], P(None, 'sec', 'blk'), may hold values from -6 to 6
- diffusivity: float32 [128, 512, 256], P('sec', 'blk'), may hold values from 0.2 to 3
- first_jacobian: float32 [5, 5], replicated, may hold values from -1.2 to 1.2
- second_jacobian: float32 [5, 5], replicated, may hold values from -1.2 to 1.2
- wall_normal: float32 [3, 128, 512], P(None, 'sec', 'blk'), may hold values from -6 to 6
- interpolation: float32 [1024, 16, 64, 64], P(('sec', 'blk')), may hold values from -0.75 to 0.75
- target_device: int32 [1024, 16], P(('sec', 'blk')), may hold values from 0 to 127, all different within a row; in each aligned block of 8 rows (0 to 7, 8 to 15, ...) at most 2 rows name the same one
- target_tile: int32 [1024, 16], P(('sec', 'blk')), may hold values from 0 to 15
- live_tiles: int32 [128], P(('sec', 'blk')), may hold values from 1 to 8, as said below
- displacement: float32 [3, 131072], P(None, ('sec', 'blk')), may hold values from -3 to 3
- stiff_diagonal: float32 [3, 131072], P(None, ('sec', 'blk')), may hold values from 1 to 1.5
- stiff_tiles: float32 [2048, 8, 64, 64], P(('sec', 'blk')), may hold values from -0.25 to 0.25
- stiff_columns: int32 [2048, 8], P(('sec', 'blk')), may hold values from 0 to 17
Outputs:
- fluid_field: float32 [5, 128, 512, 256], P(None, 'sec', 'blk')
- final_displacement: float32 [3, 131072], P(None, ('sec', 'blk'))
The draws below stay inside these ranges and needn't reach their ends.
Inputs may be any that keep to these rules, and one draw needn't show every extreme that they name: `target_device`: each row names 16 different devices; within each device's aligned block of 8 rows no device is named more than 2 times. `live_tiles`: the live tiles of a device are its first that many interface tiles. `stiff_columns`: 0 is the last tile of the device before, 1 to 16 the device's own tiles, 17 the first tile of the device after.
All inputs are finite; a program needn't handle non-finite values.
Results may differ from the reference program's by a relative error of at most 0.0001.
Values sent between devices are 32-bit elements; how exact they have to be, the bound alone decides.
No kernel may reach another device: no remote copies, remote signals or barrier semaphores. Data moves between devices by JAX's collectives and lax.ppermute only.
A program may use at most 192 MiB of HBM per device.

```python
import math
import jax
import jax.numpy as jnp
import numpy as np
from jax import lax

COMP = 5
TILE = 64
KT = 16
KB = 8
ITERS = 3
SWEEPS = 3
FX = 32
FY = 16
FZ = 256
ST = 16
GX = 128
GY = 512
FIT = 8
F_TILES = 1024
CAP = 2
S_TILES = 2048
S_NODES = 131072
N_SEC = 4
N_BLK = 32
DEVICES = 128


def draw_live_tiles(key, part):
    lowest = FIT - FIT // 4
    counts = jax.random.randint(jax.random.fold_in(key, 11), (DEVICES,), lowest, FIT + 1, dtype=jnp.int32)
    shuffled = jax.random.permutation(jax.random.fold_in(key, 12), DEVICES)
    counts = counts.at[shuffled[0]].set(FIT)
    counts = counts.at[shuffled[1]].set(1)
    return counts.astype(jnp.int32)


def set_ends(entries, rng, low, largest):
    longest = entries.shape.index(max(entries.shape))
    spots = []
    for shift in (0, 1):
        where = [jax.random.randint(jax.random.fold_in(rng, axis), (), 0, length) for axis, length in enumerate(entries.shape)]
        where[longest] = (where[longest] + shift) % entries.shape[longest]
        spots.append(tuple(where))
    return entries.at[spots[0]].set(low).at[spots[1]].set(largest)


def steps_of(own_key, shape, pieces, least, largest):
    loudness, own = 1.0, jax.random.fold_in(own_key, 6)
    for dim, parts in pieces:
        steps = jnp.exp(jax.random.uniform(jax.random.fold_in(own, dim), (parts,), jnp.float32, least / len(pieces), largest / len(pieces)))
        loudness = loudness * jnp.repeat(steps, shape[dim] // parts).reshape([-1 if axis == dim else 1 for axis in range(len(shape))])
    return loudness


def assign_block(own_key, own, number, rows, count, top, bound, lean):
    sequence = jax.random.permutation(own_key, count)
    crowded, ordinary = shares(count, rows * top, bound, lean, True), shares(count, rows * top, bound, lean, False)
    places = jnp.arange(count)

    def named(sizes, rotation):
        used = int((sizes > 0).sum())
        fixed = max(1, used // 4)
        shifted = fixed + (places - fixed + rotation * (used - fixed)) % max(1, count - fixed)
        return jnp.zeros((count,), jnp.int32).at[sequence[jnp.where(places < fixed, places, shifted)]].set(jnp.asarray(sizes, jnp.int32))

    sizes = jnp.where(number % 4 == 0, named(crowded, number // 4), named(ordinary, number - number // 4 - 1))
    mixed = jax.random.permutation(jax.random.fold_in(own, 3), count)
    source_of, taker = mixed[0:count // 2 * 2:2], mixed[1:count // 2 * 2:2]
    slack = jnp.minimum(sizes[source_of] - 1, bound - sizes[taker]) // 2
    slack = jnp.where((source_of == sequence[0]) | (taker == sequence[0]) | (sizes[taker] == 0), 0, jnp.maximum(slack, 0))
    shifted = jax.random.randint(jax.random.fold_in(own, 4), (count // 2,), 0, 1 << 20) % (slack + 1)
    sizes = sizes.at[source_of].add(-shifted).at[taker].add(shifted)
    items = jnp.searchsorted(jnp.cumsum(sizes), jnp.arange(rows * top), side="right").astype(jnp.int32)
    listing = items.reshape(top, rows).T
    listing = listing[jax.random.permutation(jax.random.fold_in(own, 1), rows)]
    rotation = jax.random.randint(jax.random.fold_in(own, 2), (rows, 1), 0, top)
    return jnp.take_along_axis(listing, (jnp.arange(top)[None, :] + rotation) % top, axis=1)


def shares(amount, total, bound, skew, full):
    loads = [(1 << 20) // math.isqrt(standing ** skew) + 1 for standing in range(1, amount + 1)]
    largest = bound if full else min(bound, max(-(-total // amount), total * loads[0] // sum(loads)))
    least = 1 if total - largest >= amount - 1 else 0
    given, rest = [largest] + [least] * (amount - 1), total - largest - least * (amount - 1)
    while rest > 0:
        movable = [i for i in range(1, amount) if given[i] < largest] or [i for i in range(1, amount) if given[i] < bound]
        whole, left = sum([loads[i] for i in movable]), rest
        for i in movable:
            extra = min(bound - given[i], max(1, left * loads[i] // whole), rest)
            given[i] = given[i] + extra
            rest = rest - extra
    return np.array(given)


def gaussian(own_key, shape, deviation, reach, shards=(), held_as=jnp.bfloat16):
    drawn = deviation * jax.random.normal(own_key, shape, jnp.float32)
    if shards:
        drawn = drawn * steps_of(own_key, shape, shards, -0.22, 0.18)
    return jnp.clip(drawn, -reach, reach).astype(held_as)


def setup_inputs(seed: int = 0) -> dict:
    key_of = jax.random.split(jax.random.key(seed), 14)
    fluid_state = gaussian(key_of[0], (COMP, GX, GY, FZ), 1.0, 6.0, ((1, 4), (2, 32)), jnp.float32)
    diffusivity = jnp.clip(jnp.exp(math.log(3.0) - 2.7080502 * jax.random.uniform(key_of[1], (GX, GY, FZ), jnp.float32) ** steps_of(key_of[1], (GX, GY, FZ), ((0, 4), (1, 32)), -0.2, 0.2)), 0.2, 3.0)
    first_jacobian = gaussian(key_of[2], (COMP, COMP), 0.3, 1.2, (), jnp.float32)
    second_jacobian = gaussian(key_of[3], (COMP, COMP), 0.3, 1.2, (), jnp.float32)
    wall_normal = gaussian(key_of[4], (3, GX, GY), 1.0, 6.0, ((1, 4), (2, 32)), jnp.float32)
    interpolation = gaussian(key_of[5], (F_TILES, KT, TILE, TILE), TILE ** -0.5, 0.75, ((0, 128),), jnp.float32)
    target_device_keys = jax.random.split(jax.random.fold_in(key_of[6], 1), F_TILES // FIT)
    target_device_turns = jax.random.permutation(jax.random.fold_in(key_of[6], 3), F_TILES // FIT)
    target_device = jax.vmap(lambda own, number: assign_block(jax.random.fold_in(key_of[6], 2), own, number, FIT, DEVICES, KT, CAP, 2))(target_device_keys, target_device_turns).reshape((F_TILES, KT))
    target_tile = set_ends(jax.random.randint(key_of[7], (F_TILES, KT), 0, ST), jax.random.fold_in(key_of[7], 1), 0, ST - 1).astype(jnp.int32)
    live_tiles = draw_live_tiles(jax.random.fold_in(key_of[13], 71), 0)
    displacement = gaussian(key_of[9], (3, S_NODES), 0.5, 3.0, ((1, 128),), jnp.float32)
    stiff_diagonal = jnp.clip(jnp.exp(math.log(1.5) - 0.4054651 * jax.random.uniform(key_of[10], (3, S_NODES), jnp.float32) ** steps_of(key_of[10], (3, S_NODES), ((1, 128),), -0.2, 0.2)), 1.0, 1.5)
    stiff_tiles = gaussian(key_of[11], (S_TILES, KB, TILE, TILE), (5 * KB * TILE // 4) ** -0.5, 0.25, ((0, 128),), jnp.float32)
    stiff_columns = set_ends(jax.random.randint(key_of[12], (S_TILES, KB), 0, ST + 2), jax.random.fold_in(key_of[12], 1), 0, (ST + 2) - 1).astype(jnp.int32)
    return {"fluid_state": fluid_state, "diffusivity": diffusivity, "first_jacobian": first_jacobian, "second_jacobian": second_jacobian, "wall_normal": wall_normal, "interpolation": interpolation, "target_device": target_device, "target_tile": target_tile, "live_tiles": live_tiles, "displacement": displacement, "stiff_diagonal": stiff_diagonal, "stiff_tiles": stiff_tiles, "stiff_columns": stiff_columns}


TIME_STEP = 0.04
RELAXATION = 0.5


def tiled_plane(plane):
    blocks = plane.reshape(3, N_SEC, FX, N_BLK, FY).transpose(1, 3, 0, 2, 4)
    blocks = blocks.reshape(N_SEC, N_BLK, 3, FIT, TILE).transpose(0, 1, 3, 2, 4)
    return blocks.reshape(F_TILES, 3, TILE)


def untiled_plane(tiles):
    blocks = tiles.reshape(N_SEC, N_BLK, FIT, 3, TILE).transpose(0, 1, 3, 2, 4)
    blocks = blocks.reshape(N_SEC, N_BLK, 3, FX, FY).transpose(2, 0, 3, 1, 4)
    return blocks.reshape(3, GX, GY)


def flux_operator(field, diffusivity, first_jacobian, second_jacobian, ghost_plane):
    padded = jnp.pad(field, ((0, 0), (1, 1), (1, 1), (0, 0)))
    east_side = padded[:, 2:, 1:-1]
    west_side = padded[:, :-2, 1:-1]
    north_side = padded[:, 1:-1, 2:]
    south_side = padded[:, 1:-1, :-2]
    zero_layer = jnp.zeros(field.shape[:-1] + (1,), jnp.float32)
    upper_side = jnp.concatenate([field[..., 1:], zero_layer], axis=3)
    lower_side = jnp.concatenate([ghost_plane[..., None], field[..., :-1]], axis=3)
    laplace = east_side + west_side + north_side + south_side + upper_side + lower_side - 6.0 * field
    first_flux = jnp.einsum("cd,dxyz->cxyz", first_jacobian, 0.5 * (east_side - west_side), precision=lax.Precision.HIGHEST)
    second_flux = jnp.einsum("cd,dxyz->cxyz", second_jacobian, 0.5 * (north_side - south_side), precision=lax.Precision.HIGHEST)
    return diffusivity[None] * laplace - first_flux - second_flux


def off_diagonal(values, stiff_tiles, window_index):
    shell_blocks = values.reshape(3, S_TILES, TILE)
    padded = jnp.pad(shell_blocks, ((0, 0), (1, 1), (0, 0)))
    gathered = padded[:, window_index]
    result = jnp.einsum("ibmn,cibn->cim", stiff_tiles, gathered, precision=lax.Precision.HIGHEST)
    return result.reshape(3, S_NODES)


def reference(fluid_state, diffusivity, first_jacobian, second_jacobian, wall_normal, interpolation, target_device, target_tile, live_tiles, displacement, stiff_diagonal, stiff_tiles, stiff_columns):
    tile_number = jnp.arange(F_TILES, dtype=jnp.int32)
    live_mask = ((tile_number % FIT) < jnp.repeat(live_tiles, FIT)).astype(jnp.float32)
    target = (target_device * ST + target_tile).astype(jnp.int32)
    owner_start = ((jnp.arange(S_TILES, dtype=jnp.int32) // ST) * ST).astype(jnp.int32)
    window_index = (owner_start[:, None] + stiff_columns).astype(jnp.int32)
    empty_plane = jnp.zeros((1, GX, GY), jnp.float32)
    current = displacement
    fluid_field = fluid_state
    for iteration in range(ITERS):
        shell_blocks = current.reshape(3, S_TILES, TILE)
        picked = shell_blocks[:, target]
        motion = jnp.einsum("rkqn,crkn->rcq", interpolation, picked, precision=lax.Precision.HIGHEST)
        motion = motion * live_mask[:, None, None]
        ghost_plane = jnp.concatenate([empty_plane, untiled_plane(motion), empty_plane], axis=0)
        first_section = fluid_state + TIME_STEP * flux_operator(fluid_state, diffusivity, first_jacobian, second_jacobian, ghost_plane)
        fluid_field = 0.5 * (fluid_state + first_section + TIME_STEP * flux_operator(first_section, diffusivity, first_jacobian, second_jacobian, ghost_plane))
        traction = wall_normal * fluid_field[4, :, :, 0][None]
        traction_tiles = tiled_plane(traction)
        contribution = jnp.einsum("rkqn,rcq->rkcn", interpolation, traction_tiles, precision=lax.Precision.HIGHEST)
        contribution = contribution * live_mask[:, None, None, None]
        forces = jax.ops.segment_sum(contribution.reshape(F_TILES * KT, 3, TILE), target.reshape(F_TILES * KT), num_segments=S_TILES)
        forces = forces.transpose(1, 0, 2).reshape(3, S_NODES)
        estimate = current
        for sweep_index in range(SWEEPS):
            estimate = (forces - off_diagonal(estimate, stiff_tiles, window_index)) / stiff_diagonal
        current = (1.0 - RELAXATION) * current + RELAXATION * estimate
    return fluid_field, current
```

```python
import jax
import jax.numpy as jnp
from jax import lax
from jax.sharding import PartitionSpec as P

ITERS = 3
SWEEPS = 3


TIME_STEP = 0.04
RELAXATION = 0.5
HIGHEST = lax.Precision.HIGHEST


def with_halo(array, sides, width):
    for axis, dim in sides:
        size, length = (lax.axis_size(axis), array.shape[dim])
        up = [(i, (i + 1) % size) for i in range(size - 1)]
        down = [(j, i) for i, j in up]
        last = lax.slice_in_dim(array, length - width, length, axis=dim)
        first = lax.slice_in_dim(array, 0, width, axis=dim)
        before = lax.ppermute(last, axis, up)
        after = lax.ppermute(first, axis, down)
        array = jnp.concatenate([before, array, after], axis=dim)
    return array


def homogeneous(padded, diffusivity, first_jacobian, second_jacobian):
    centre = padded[:, 1:-1, 1:-1]
    east_side = padded[:, 2:, 1:-1]
    west_side = padded[:, :-2, 1:-1]
    north_side = padded[:, 1:-1, 2:]
    south_side = padded[:, 1:-1, :-2]
    zero_layer = jnp.zeros(centre.shape[:-1] + (1,), jnp.float32)
    upper_side = jnp.concatenate([centre[..., 1:], zero_layer], axis=3)
    lower_side = jnp.concatenate([zero_layer, centre[..., :-1]], axis=3)
    laplace = (
        east_side + west_side + north_side + south_side + upper_side + lower_side - 6.0 * centre
    )
    first_flux = jnp.einsum(
        "cd,dxyz->cxyz", first_jacobian, 0.5 * (east_side - west_side), precision=HIGHEST
    )
    second_flux = jnp.einsum(
        "cd,dxyz->cxyz", second_jacobian, 0.5 * (north_side - south_side), precision=HIGHEST
    )
    return diffusivity[None] * laplace - first_flux - second_flux


def face_rim(field):
    return with_halo(field, (("sec", 1), ("blk", 2)), 1)


def plane_sides(plane):
    sides = []
    for axis, dim in (("sec", 1), ("blk", 2)):
        size, length = (lax.axis_size(axis), plane.shape[dim])
        up = [(i, i + 1) for i in range(size - 1)]
        down = [(j, i) for i, j in up]
        before = lax.ppermute(lax.slice_in_dim(plane, length - 1, length, axis=dim), axis, up)
        after = lax.ppermute(lax.slice_in_dim(plane, 0, 1, axis=dim), axis, down)
        ahead = jnp.concatenate([lax.slice_in_dim(plane, 1, length, axis=dim), after], axis=dim)
        behind = jnp.concatenate([before, lax.slice_in_dim(plane, 0, length - 1, axis=dim)], axis=dim)
        sides.append((ahead, behind))
    return sides


def local(
    fluid_state,
    diffusivity,
    first_jacobian,
    second_jacobian,
    wall_normal,
    interpolation,
    target_device,
    target_tile,
    live_tiles,
    displacement,
    stiff_diagonal,
    stiff_tiles,
    stiff_columns,
):
    devices = lax.axis_size(("sec", "blk"))
    wall_tiles = interpolation.shape[0]
    fan_tiles = interpolation.shape[1]
    tile_size = interpolation.shape[2]
    slots_each = 2 * wall_tiles * fan_tiles // devices
    total_slots = devices * slots_each
    pair_count = wall_tiles * fan_tiles
    shell_tiles = displacement.shape[1] // tile_size
    rows_first = fluid_state.shape[1]
    rows_second = fluid_state.shape[2]
    destination = target_device.reshape(pair_count)
    position = jnp.arange(pair_count, dtype=jnp.int32)
    earlier = (destination[:, None] == destination[None, :]) & (
        position[None, :] < position[:, None]
    )
    rank_within = jnp.sum(earlier.astype(jnp.int32), axis=1)
    slot_index = destination * slots_each + rank_within
    slot_match = slot_index[:, None] == jnp.arange(total_slots, dtype=jnp.int32)[None, :]
    slot_table = slot_match.astype(jnp.float32)
    tile_plus = target_tile.reshape(pair_count) + 1
    sent_tiles = jnp.sum(jnp.where(slot_match, tile_plus[:, None], 0), axis=0) - 1
    owned_tiles = lax.all_to_all(
        sent_tiles.reshape(devices, slots_each),
        ("sec", "blk"),
        split_axis=0,
        concat_axis=0,
        tiled=True,
    ).reshape(total_slots)
    owner_table = (
        owned_tiles[:, None] == jnp.arange(shell_tiles, dtype=jnp.int32)[None, :]
    ).astype(jnp.float32)
    live_mask = (jnp.arange(wall_tiles, dtype=jnp.int32) < live_tiles[0]).astype(jnp.float32)
    column_table = (
        stiff_columns[:, :, None] == jnp.arange(shell_tiles + 2, dtype=jnp.int32)[None, None, :]
    ).astype(jnp.float32)

    def send_forth(buffer):
        arrived = lax.all_to_all(buffer, ("sec", "blk"), split_axis=0, concat_axis=0, tiled=True)
        return arrived

    def shell_forces(wall_value):
        traction = wall_normal * wall_value[None]
        traction_tiles = traction.reshape(3, wall_tiles, tile_size)
        contribution = jnp.einsum(
            "rkqn,crq->rkcn", interpolation, traction_tiles, precision=HIGHEST
        )
        contribution = contribution * live_mask[:, None, None, None]
        outgoing = jnp.einsum(
            "pm,pcn->mcn",
            slot_table,
            contribution.reshape(pair_count, 3, tile_size),
            precision=HIGHEST,
        )
        arrived = send_forth(outgoing.reshape(devices, slots_each, 3, tile_size)).reshape(
            total_slots, 3, tile_size
        )
        forces = jnp.einsum("ms,mcn->csn", owner_table, arrived, precision=HIGHEST)
        return forces.reshape(3, shell_tiles * tile_size)

    def off_diagonal(values):
        window = with_halo(values, ((("sec", "blk"), 1),), tile_size)
        window_tiles = window.reshape(3, shell_tiles + 2, tile_size)
        chosen = jnp.einsum("ibj,cjn->ibcn", column_table, window_tiles, precision=HIGHEST)
        result = jnp.einsum("ibmn,ibcn->cim", stiff_tiles, chosen, precision=HIGHEST)
        return result.reshape(3, shell_tiles * tile_size)

    def shell_update(current, wall_value):
        forces = shell_forces(wall_value)
        estimate = current
        for sweep_index in range(SWEEPS):
            estimate = (forces - off_diagonal(estimate)) / stiff_diagonal
        return (1.0 - RELAXATION) * current + RELAXATION * estimate

    wall_bottom = diffusivity[:, :, 0]
    wall_above = diffusivity[:, :, 1]
    first_section = fluid_state + TIME_STEP * homogeneous(
        face_rim(fluid_state), diffusivity, first_jacobian, second_jacobian
    )
    settled = 0.5 * (
        fluid_state
        + first_section
        + TIME_STEP
        * homogeneous(face_rim(first_section), diffusivity, first_jacobian, second_jacobian)
    )
    settled_wall = settled[4, :, :, 0]
    half_square = 0.5 * TIME_STEP * TIME_STEP

    def wall_state(motion_plane):
        source = motion_plane * wall_bottom[None]
        (east_side, west_side), (north_side, south_side) = plane_sides(source)
        first_flux = jnp.einsum(
            "cd,dxy->cxy", first_jacobian[:, 1:4], 0.5 * (east_side - west_side), precision=HIGHEST
        )
        second_flux = jnp.einsum(
            "cd,dxy->cxy", second_jacobian[:, 1:4], 0.5 * (north_side - south_side), precision=HIGHEST
        )
        return source, east_side + west_side + north_side + south_side, first_flux, second_flux

    current = displacement
    for iteration in range(ITERS):
        shell_blocks = current.reshape(3, shell_tiles, tile_size)
        reply_tiles = jnp.einsum("ms,csn->mcn", owner_table, shell_blocks, precision=HIGHEST)
        returned = lax.all_to_all(
            reply_tiles.reshape(devices, slots_each, 3, tile_size),
            ("sec", "blk"),
            split_axis=0,
            concat_axis=0,
            tiled=True,
        )
        interface_returned = returned.reshape(total_slots, 3, tile_size)
        pair_values = jnp.einsum("pm,mcn->pcn", slot_table, interface_returned, precision=HIGHEST)
        pair_values = pair_values.reshape(wall_tiles, fan_tiles, 3, tile_size)
        motion = (
            jnp.einsum("rkqn,rkcn->rcq", interpolation, pair_values, precision=HIGHEST)
            * live_mask[:, None, None]
        )
        motion_plane = motion.transpose(1, 0, 2).reshape(3, rows_first, rows_second)
        source, neighbours, first_flux, second_flux = wall_state(motion_plane)
        wall_value = settled_wall - half_square * (first_flux[4] + second_flux[4])
        current = shell_update(current, wall_value)
    bottom = TIME_STEP * source + half_square * (
        wall_bottom[None] * (neighbours - 6.0 * source) - first_flux[1:4] - second_flux[1:4]
    )
    above = half_square * wall_above[None] * source
    zero_plane = jnp.zeros_like(source[:1])
    bottom = jnp.concatenate([zero_plane, bottom, zero_plane], axis=0)
    bottom = bottom.at[0].add(-half_square * (first_flux[0] + second_flux[0]))
    bottom = bottom.at[4].add(-half_square * (first_flux[4] + second_flux[4]))
    above = jnp.concatenate([zero_plane, above, zero_plane], axis=0)
    edge = jnp.stack([bottom, above], axis=3)
    fluid_field = lax.dynamic_update_slice(
        settled, settled[:, :, :, 0:2] + edge, (0, 0, 0, 0)
    )
    return (fluid_field, current)


def solution(mesh):
    return jax.shard_map(
        local,
        mesh=mesh,
        in_specs=(
            P(None, "sec", "blk", None),
            P("sec", "blk", None),
            P(),
            P(),
            P(None, "sec", "blk"),
            P(("sec", "blk"), None, None, None),
            P(("sec", "blk"), None),
            P(("sec", "blk"), None),
            P(("sec", "blk")),
            P(None, ("sec", "blk")),
            P(None, ("sec", "blk")),
            P(("sec", "blk"), None, None, None),
            P(("sec", "blk"), None),
        ),
        out_specs=(P(None, "sec", "blk", None), P(None, ("sec", "blk"))),
        check_vma=False,
    )
```

```python
import jax
import jax.numpy as jnp
from jax import lax
from jax.sharding import PartitionSpec as P

ITERS = 3
SWEEPS = 3


TIME_STEP = 0.04
RELAXATION = 0.5
HIGHEST = lax.Precision.HIGHEST


def with_halo(array, sides, width):
    for axis, dim in sides:
        size, length = (lax.axis_size(axis), array.shape[dim])
        up = [(i, (i + 1) % size) for i in range(size - 1)]
        down = [(j, i) for i, j in up]
        last = lax.slice_in_dim(array, length - width, length, axis=dim)
        first = lax.slice_in_dim(array, 0, width, axis=dim)
        before = lax.ppermute(last, axis, up)
        after = lax.ppermute(first, axis, down)
        array = jnp.concatenate([before, array, after], axis=dim)
    return array


def homogeneous(padded, diffusivity, first_jacobian, second_jacobian):
    centre = padded[:, 1:-1, 1:-1]
    east_side = padded[:, 2:, 1:-1]
    west_side = padded[:, :-2, 1:-1]
    north_side = padded[:, 1:-1, 2:]
    south_side = padded[:, 1:-1, :-2]
    zero_layer = jnp.zeros(centre.shape[:-1] + (1,), jnp.float32)
    upper_side = jnp.concatenate([centre[..., 1:], zero_layer], axis=3)
    lower_side = jnp.concatenate([zero_layer, centre[..., :-1]], axis=3)
    laplace = (
        east_side + west_side + north_side + south_side + upper_side + lower_side - 6.0 * centre
    )
    first_step = 0.5 * (east_side - west_side)
    second_step = 0.5 * (north_side - south_side)
    return (
        diffusivity[None] * laplace
        - blended(first_jacobian, first_step)
        - blended(second_jacobian, second_step)
    )


def blended(jacobian, values):
    total = jacobian[:, 0, None, None, None] * values[0][None]
    for d in range(1, values.shape[0]):
        total = total + jacobian[:, d, None, None, None] * values[d][None]
    return total


def mixed(jacobian, row, values):
    total = jacobian[row, 0] * values[0]
    for d in range(1, values.shape[0]):
        total = total + jacobian[row, d] * values[d]
    return total


def face_rim(field):
    return with_halo(field, (("sec", 1), ("blk", 2)), 1)


def plane_sides(plane):
    sides = []
    for axis, dim in (("sec", 1), ("blk", 2)):
        size, length = (lax.axis_size(axis), plane.shape[dim])
        up = [(i, i + 1) for i in range(size - 1)]
        down = [(j, i) for i, j in up]
        before = lax.ppermute(lax.slice_in_dim(plane, length - 1, length, axis=dim), axis, up)
        after = lax.ppermute(lax.slice_in_dim(plane, 0, 1, axis=dim), axis, down)
        ahead = jnp.concatenate([lax.slice_in_dim(plane, 1, length, axis=dim), after], axis=dim)
        behind = jnp.concatenate([before, lax.slice_in_dim(plane, 0, length - 1, axis=dim)], axis=dim)
        sides.append((ahead, behind))
    return sides


def local(
    fluid_state,
    diffusivity,
    first_jacobian,
    second_jacobian,
    wall_normal,
    interpolation,
    target_device,
    target_tile,
    live_tiles,
    displacement,
    stiff_diagonal,
    stiff_tiles,
    stiff_columns,
):
    devices = lax.axis_size(("sec", "blk"))
    wall_tiles = interpolation.shape[0]
    fan_tiles = interpolation.shape[1]
    tile_size = interpolation.shape[2]
    slots_each = 2 * wall_tiles * fan_tiles // devices
    total_slots = devices * slots_each
    pair_count = wall_tiles * fan_tiles
    shell_tiles = displacement.shape[1] // tile_size
    rows_first = fluid_state.shape[1]
    rows_second = fluid_state.shape[2]
    destination = target_device.reshape(pair_count)
    position = jnp.arange(pair_count, dtype=jnp.int32)
    earlier = (destination[:, None] == destination[None, :]) & (
        position[None, :] < position[:, None]
    )
    rank_within = jnp.sum(earlier.astype(jnp.int32), axis=1)
    slot_index = destination * slots_each + rank_within
    slot_match = slot_index[:, None] == jnp.arange(total_slots, dtype=jnp.int32)[None, :]
    slot_table = slot_match.astype(jnp.float32)
    tile_plus = target_tile.reshape(pair_count) + 1
    sent_tiles = jnp.sum(jnp.where(slot_match, tile_plus[:, None], 0), axis=0) - 1
    owned_tiles = lax.all_to_all(
        sent_tiles.reshape(devices, slots_each),
        ("sec", "blk"),
        split_axis=0,
        concat_axis=0,
        tiled=True,
    ).reshape(total_slots)
    owner_table = (
        owned_tiles[:, None] == jnp.arange(shell_tiles, dtype=jnp.int32)[None, :]
    ).astype(jnp.float32)
    live_mask = (jnp.arange(wall_tiles, dtype=jnp.int32) < live_tiles[0]).astype(jnp.float32)
    column_table = (
        stiff_columns[:, :, None] == jnp.arange(shell_tiles + 2, dtype=jnp.int32)[None, None, :]
    ).astype(jnp.float32)

    def send_forth(buffer):
        arrived = lax.all_to_all(buffer, ("sec", "blk"), split_axis=0, concat_axis=0, tiled=True)
        return arrived

    def shell_forces(wall_value):
        traction = wall_normal * wall_value[None]
        traction_tiles = traction.reshape(3, wall_tiles, tile_size)
        contribution = jnp.einsum(
            "rkqn,crq->rkcn", interpolation, traction_tiles, precision=HIGHEST
        )
        contribution = contribution * live_mask[:, None, None, None]
        outgoing = jnp.einsum(
            "pm,pcn->mcn",
            slot_table,
            contribution.reshape(pair_count, 3, tile_size),
            precision=HIGHEST,
        )
        arrived = send_forth(outgoing.reshape(devices, slots_each, 3, tile_size)).reshape(
            total_slots, 3, tile_size
        )
        forces = jnp.einsum("ms,mcn->csn", owner_table, arrived, precision=HIGHEST)
        return forces.reshape(3, shell_tiles * tile_size)

    def off_diagonal(values):
        window = with_halo(values, ((("sec", "blk"), 1),), tile_size)
        window_tiles = window.reshape(3, shell_tiles + 2, tile_size)
        chosen = jnp.einsum("ibj,cjn->ibcn", column_table, window_tiles, precision=HIGHEST)
        result = jnp.einsum("ibmn,ibcn->cim", stiff_tiles, chosen, precision=HIGHEST)
        return result.reshape(3, shell_tiles * tile_size)

    def shell_update(current, wall_value):
        forces = shell_forces(wall_value)
        estimate = current
        for sweep_index in range(SWEEPS):
            estimate = (forces - off_diagonal(estimate)) / stiff_diagonal
        return (1.0 - RELAXATION) * current + RELAXATION * estimate

    wall_bottom = diffusivity[:, :, 0]
    wall_above = diffusivity[:, :, 1]
    first_section = fluid_state + TIME_STEP * homogeneous(
        face_rim(fluid_state), diffusivity, first_jacobian, second_jacobian
    )
    settled = 0.5 * (
        fluid_state
        + first_section
        + TIME_STEP
        * homogeneous(face_rim(first_section), diffusivity, first_jacobian, second_jacobian)
    )
    settled = lax.optimization_barrier(settled)
    settled_wall = settled[4, :, :, 0]
    half_square = 0.5 * TIME_STEP * TIME_STEP
    edge_rows = jnp.array([1.0, 0.0, 0.0, 0.0, 1.0], jnp.float32)

    def wall_state(motion_plane):
        source = motion_plane * wall_bottom[None]
        (east_side, west_side), (north_side, south_side) = plane_sides(source)
        first_step = 0.5 * (east_side - west_side)
        second_step = 0.5 * (north_side - south_side)
        first_flux = jnp.stack([mixed(first_jacobian[:, 1:4], c, first_step) for c in range(5)])
        second_flux = jnp.stack([mixed(second_jacobian[:, 1:4], c, second_step) for c in range(5)])
        return source, east_side + west_side + north_side + south_side, first_flux, second_flux

    current = displacement
    for iteration in range(ITERS):
        shell_blocks = current.reshape(3, shell_tiles, tile_size)
        reply_tiles = jnp.einsum("ms,csn->mcn", owner_table, shell_blocks, precision=HIGHEST)
        returned = lax.all_to_all(
            reply_tiles.reshape(devices, slots_each, 3, tile_size),
            ("sec", "blk"),
            split_axis=0,
            concat_axis=0,
            tiled=True,
        )
        interface_returned = returned.reshape(total_slots, 3, tile_size)
        pair_values = jnp.einsum("pm,mcn->pcn", slot_table, interface_returned, precision=HIGHEST)
        pair_values = pair_values.reshape(wall_tiles, fan_tiles, 3, tile_size)
        motion = (
            jnp.einsum("rkqn,rkcn->rcq", interpolation, pair_values, precision=HIGHEST)
            * live_mask[:, None, None]
        )
        motion_plane = motion.transpose(1, 0, 2).reshape(3, rows_first, rows_second)
        source, neighbours, first_flux, second_flux = wall_state(motion_plane)
        wall_value = settled_wall - half_square * (first_flux[4] + second_flux[4])
        current = shell_update(current, wall_value)
    bottom = TIME_STEP * source + half_square * (
        wall_bottom[None] * (neighbours - 6.0 * source) - first_flux[1:4] - second_flux[1:4]
    )
    above = half_square * wall_above[None] * source
    zero_plane = jnp.zeros_like(source[:1])
    bottom = jnp.concatenate([zero_plane, bottom, zero_plane], axis=0)
    bottom = bottom - half_square * (first_flux + second_flux) * edge_rows[:, None, None]
    above = jnp.concatenate([zero_plane, above, zero_plane], axis=0)
    depth = lax.broadcasted_iota(jnp.int32, settled.shape, 3)
    fluid_field = settled + jnp.where(
        depth == 0, bottom[..., None], jnp.where(depth == 1, above[..., None], 0.0)
    )
    return (fluid_field, current)


def solution(mesh):
    return jax.shard_map(
        local,
        mesh=mesh,
        in_specs=(
            P(None, "sec", "blk", None),
            P("sec", "blk", None),
            P(),
            P(),
            P(None, "sec", "blk"),
            P(("sec", "blk"), None, None, None),
            P(("sec", "blk"), None),
            P(("sec", "blk"), None),
            P(("sec", "blk")),
            P(None, ("sec", "blk")),
            P(None, ("sec", "blk")),
            P(("sec", "blk"), None, None, None),
            P(("sec", "blk"), None),
        ),
        out_specs=(P(None, "sec", "blk", None), P(None, ("sec", "blk"))),
        check_vma=False,
    )
```

```python
import jax
import jax.numpy as jnp
from jax import lax
from jax.sharding import PartitionSpec as P

ITERS = 3
SWEEPS = 3


TIME_STEP = 0.04
RELAXATION = 0.5
HIGHEST = lax.Precision.HIGHEST
HIGH = lax.Precision.HIGH


def with_halo(array, sides, width):
    for axis, dim in sides:
        size, length = (lax.axis_size(axis), array.shape[dim])
        up = [(i, (i + 1) % size) for i in range(size - 1)]
        down = [(j, i) for i, j in up]
        last = lax.slice_in_dim(array, length - width, length, axis=dim)
        first = lax.slice_in_dim(array, 0, width, axis=dim)
        before = lax.ppermute(last, axis, up)
        after = lax.ppermute(first, axis, down)
        array = jnp.concatenate([before, array, after], axis=dim)
    return array


def homogeneous(padded, diffusivity, first_jacobian, second_jacobian):
    centre = padded[:, 1:-1, 1:-1]
    east_side = padded[:, 2:, 1:-1]
    west_side = padded[:, :-2, 1:-1]
    north_side = padded[:, 1:-1, 2:]
    south_side = padded[:, 1:-1, :-2]
    zero_layer = jnp.zeros(centre.shape[:-1] + (1,), jnp.float32)
    upper_side = jnp.concatenate([centre[..., 1:], zero_layer], axis=3)
    lower_side = jnp.concatenate([zero_layer, centre[..., :-1]], axis=3)
    laplace = (
        east_side + west_side + north_side + south_side + upper_side + lower_side - 6.0 * centre
    )
    first_flux = jnp.einsum(
        "cd,dxyz->cxyz", first_jacobian, 0.5 * (east_side - west_side), precision=HIGH
    )
    second_flux = jnp.einsum(
        "cd,dxyz->cxyz", second_jacobian, 0.5 * (north_side - south_side), precision=HIGH
    )
    return diffusivity[None] * laplace - first_flux - second_flux


def mixed(jacobian, row, values):
    total = jacobian[row, 0] * values[0]
    for d in range(1, values.shape[0]):
        total = total + jacobian[row, d] * values[d]
    return total


def face_rim(field):
    return with_halo(field, (("sec", 1), ("blk", 2)), 1)


def plane_sides(plane):
    sides = []
    for axis, dim in (("sec", 1), ("blk", 2)):
        size, length = (lax.axis_size(axis), plane.shape[dim])
        up = [(i, i + 1) for i in range(size - 1)]
        down = [(j, i) for i, j in up]
        before = lax.ppermute(lax.slice_in_dim(plane, length - 1, length, axis=dim), axis, up)
        after = lax.ppermute(lax.slice_in_dim(plane, 0, 1, axis=dim), axis, down)
        ahead = jnp.concatenate([lax.slice_in_dim(plane, 1, length, axis=dim), after], axis=dim)
        behind = jnp.concatenate([before, lax.slice_in_dim(plane, 0, length - 1, axis=dim)], axis=dim)
        sides.append((ahead, behind))
    return sides


def local(
    fluid_state,
    diffusivity,
    first_jacobian,
    second_jacobian,
    wall_normal,
    interpolation,
    target_device,
    target_tile,
    live_tiles,
    displacement,
    stiff_diagonal,
    stiff_tiles,
    stiff_columns,
):
    devices = lax.axis_size(("sec", "blk"))
    wall_tiles = interpolation.shape[0]
    fan_tiles = interpolation.shape[1]
    tile_size = interpolation.shape[2]
    slots_each = 2 * wall_tiles * fan_tiles // devices
    total_slots = devices * slots_each
    pair_count = wall_tiles * fan_tiles
    shell_tiles = displacement.shape[1] // tile_size
    rows_first = fluid_state.shape[1]
    rows_second = fluid_state.shape[2]
    destination = target_device.reshape(pair_count)
    position = jnp.arange(pair_count, dtype=jnp.int32)
    earlier = (destination[:, None] == destination[None, :]) & (
        position[None, :] < position[:, None]
    )
    rank_within = jnp.sum(earlier.astype(jnp.int32), axis=1)
    slot_index = destination * slots_each + rank_within
    slot_match = slot_index[:, None] == jnp.arange(total_slots, dtype=jnp.int32)[None, :]
    slot_table = slot_match.astype(jnp.float32)
    tile_plus = target_tile.reshape(pair_count) + 1
    sent_tiles = jnp.sum(jnp.where(slot_match, tile_plus[:, None], 0), axis=0) - 1
    owned_tiles = lax.all_to_all(
        sent_tiles.reshape(devices, slots_each),
        ("sec", "blk"),
        split_axis=0,
        concat_axis=0,
        tiled=True,
    ).reshape(total_slots)
    owner_table = (
        owned_tiles[:, None] == jnp.arange(shell_tiles, dtype=jnp.int32)[None, :]
    ).astype(jnp.float32)
    live_mask = (jnp.arange(wall_tiles, dtype=jnp.int32) < live_tiles[0]).astype(jnp.float32)
    column_table = (
        stiff_columns[:, :, None] == jnp.arange(shell_tiles + 2, dtype=jnp.int32)[None, None, :]
    ).astype(jnp.float32)

    def send_forth(buffer):
        arrived = lax.all_to_all(buffer, ("sec", "blk"), split_axis=0, concat_axis=0, tiled=True)
        return arrived

    def shell_forces(wall_value):
        traction = wall_normal * wall_value[None]
        traction_tiles = traction.reshape(3, wall_tiles, tile_size)
        contribution = jnp.einsum(
            "rkqn,crq->rkcn", interpolation, traction_tiles, precision=HIGH
        )
        contribution = contribution * live_mask[:, None, None, None]
        outgoing = jnp.einsum(
            "pm,pcn->mcn",
            slot_table,
            contribution.reshape(pair_count, 3, tile_size),
            precision=HIGHEST,
        )
        arrived = send_forth(outgoing.reshape(devices, slots_each, 3, tile_size)).reshape(
            total_slots, 3, tile_size
        )
        forces = jnp.einsum("ms,mcn->csn", owner_table, arrived, precision=HIGHEST)
        return forces.reshape(3, shell_tiles * tile_size)

    def off_diagonal(values):
        window = with_halo(values, ((("sec", "blk"), 1),), tile_size)
        window_tiles = window.reshape(3, shell_tiles + 2, tile_size)
        chosen = jnp.einsum("ibj,cjn->ibcn", column_table, window_tiles, precision=HIGHEST)
        result = jnp.einsum("ibmn,ibcn->cim", stiff_tiles, chosen, precision=HIGH)
        return result.reshape(3, shell_tiles * tile_size)

    def shell_update(current, wall_value):
        forces = shell_forces(wall_value)
        estimate = current
        for sweep_index in range(SWEEPS):
            estimate = (forces - off_diagonal(estimate)) / stiff_diagonal
        return (1.0 - RELAXATION) * current + RELAXATION * estimate

    wall_bottom = diffusivity[:, :, 0]
    wall_above = diffusivity[:, :, 1]
    first_section = fluid_state + TIME_STEP * homogeneous(
        face_rim(fluid_state), diffusivity, first_jacobian, second_jacobian
    )
    settled = 0.5 * (
        fluid_state
        + first_section
        + TIME_STEP
        * homogeneous(face_rim(first_section), diffusivity, first_jacobian, second_jacobian)
    )
    settled = lax.optimization_barrier(settled)
    settled_wall = settled[4, :, :, 0]
    half_square = 0.5 * TIME_STEP * TIME_STEP
    edge_rows = jnp.array([1.0, 0.0, 0.0, 0.0, 1.0], jnp.float32)

    def wall_state(motion_plane):
        source = motion_plane * wall_bottom[None]
        (east_side, west_side), (north_side, south_side) = plane_sides(source)
        first_step = 0.5 * (east_side - west_side)
        second_step = 0.5 * (north_side - south_side)
        first_flux = jnp.stack([mixed(first_jacobian[:, 1:4], c, first_step) for c in range(5)])
        second_flux = jnp.stack([mixed(second_jacobian[:, 1:4], c, second_step) for c in range(5)])
        return source, east_side + west_side + north_side + south_side, first_flux, second_flux

    current = displacement
    for iteration in range(ITERS):
        shell_blocks = current.reshape(3, shell_tiles, tile_size)
        reply_tiles = jnp.einsum("ms,csn->mcn", owner_table, shell_blocks, precision=HIGHEST)
        returned = lax.all_to_all(
            reply_tiles.reshape(devices, slots_each, 3, tile_size),
            ("sec", "blk"),
            split_axis=0,
            concat_axis=0,
            tiled=True,
        )
        interface_returned = returned.reshape(total_slots, 3, tile_size)
        pair_values = jnp.einsum("pm,mcn->pcn", slot_table, interface_returned, precision=HIGHEST)
        pair_values = pair_values.reshape(wall_tiles, fan_tiles, 3, tile_size)
        motion = (
            jnp.einsum("rkqn,rkcn->rcq", interpolation, pair_values, precision=HIGH)
            * live_mask[:, None, None]
        )
        motion_plane = motion.transpose(1, 0, 2).reshape(3, rows_first, rows_second)
        source, neighbours, first_flux, second_flux = wall_state(motion_plane)
        wall_value = settled_wall - half_square * (first_flux[4] + second_flux[4])
        current = shell_update(current, wall_value)
    bottom = TIME_STEP * source + half_square * (
        wall_bottom[None] * (neighbours - 6.0 * source) - first_flux[1:4] - second_flux[1:4]
    )
    above = half_square * wall_above[None] * source
    zero_plane = jnp.zeros_like(source[:1])
    bottom = jnp.concatenate([zero_plane, bottom, zero_plane], axis=0)
    bottom = bottom - half_square * (first_flux + second_flux) * edge_rows[:, None, None]
    above = jnp.concatenate([zero_plane, above, zero_plane], axis=0)
    depth = lax.broadcasted_iota(jnp.int32, settled.shape, 3)
    fluid_field = settled + jnp.where(
        depth == 0, bottom[..., None], jnp.where(depth == 1, above[..., None], 0.0)
    )
    return (fluid_field, current)


def solution(mesh):
    return jax.shard_map(
        local,
        mesh=mesh,
        in_specs=(
            P(None, "sec", "blk", None),
            P("sec", "blk", None),
            P(),
            P(),
            P(None, "sec", "blk"),
            P(("sec", "blk"), None, None, None),
            P(("sec", "blk"), None),
            P(("sec", "blk"), None),
            P(("sec", "blk")),
            P(None, ("sec", "blk")),
            P(None, ("sec", "blk")),
            P(("sec", "blk"), None, None, None),
            P(("sec", "blk"), None),
        ),
        out_specs=(P(None, "sec", "blk", None), P(None, ("sec", "blk"))),
        check_vma=False,
    )
```

```python
import functools

import jax
import jax.numpy as jnp
from jax import lax
from jax.experimental import pallas as pl
from jax.experimental.pallas import tpu as pltpu
from jax.sharding import PartitionSpec as P

ITERS = 3
SWEEPS = 3


TIME_STEP = 0.04
RELAXATION = 0.5
HIGHEST = lax.Precision.HIGHEST
HIGH = lax.Precision.HIGH


def with_halo(array, sides, width):
    for axis, dim in sides:
        size, length = (lax.axis_size(axis), array.shape[dim])
        up = [(i, (i + 1) % size) for i in range(size - 1)]
        down = [(j, i) for i, j in up]
        last = lax.slice_in_dim(array, length - width, length, axis=dim)
        first = lax.slice_in_dim(array, 0, width, axis=dim)
        before = lax.ppermute(last, axis, up)
        after = lax.ppermute(first, axis, down)
        array = jnp.concatenate([before, array, after], axis=dim)
    return array


def homogeneous(padded, diffusivity, first_jacobian, second_jacobian):
    centre = padded[:, 1:-1, 1:-1]
    east_side = padded[:, 2:, 1:-1]
    west_side = padded[:, :-2, 1:-1]
    north_side = padded[:, 1:-1, 2:]
    south_side = padded[:, 1:-1, :-2]
    zero_layer = jnp.zeros(centre.shape[:-1] + (1,), jnp.float32)
    upper_side = jnp.concatenate([centre[..., 1:], zero_layer], axis=3)
    lower_side = jnp.concatenate([zero_layer, centre[..., :-1]], axis=3)
    laplace = (
        east_side + west_side + north_side + south_side + upper_side + lower_side - 6.0 * centre
    )
    first_flux = jnp.einsum(
        "cd,dxyz->cxyz", first_jacobian, 0.5 * (east_side - west_side), precision=HIGH
    )
    second_flux = jnp.einsum(
        "cd,dxyz->cxyz", second_jacobian, 0.5 * (north_side - south_side), precision=HIGH
    )
    return diffusivity[None] * laplace - first_flux - second_flux


def mixed(jacobian, row, values):
    total = jacobian[row, 0] * values[0]
    for d in range(1, values.shape[0]):
        total = total + jacobian[row, d] * values[d]
    return total


def flux_kernel(jac_ref, pad_ref, dif_ref, extra_ref, out_ref, *, keep, blend, rate):
    comps, rows, cols, depth = out_ref.shape
    lanes = lax.broadcasted_iota(jnp.int32, (cols, depth), 1)
    top = lanes == depth - 1
    bottom = lanes == 0

    def row(x, carry):
        dif = dif_ref[x]
        steps_x, steps_y, laps = [], [], []
        for d in range(comps):
            east = pad_ref[d, x + 2, pl.ds(1, cols), :]
            west = pad_ref[d, x, pl.ds(1, cols), :]
            north = pad_ref[d, x + 1, pl.ds(2, cols), :]
            south = pad_ref[d, x + 1, pl.ds(0, cols), :]
            centre = pad_ref[d, x + 1, pl.ds(1, cols), :]
            upper = jnp.where(top, 0.0, pltpu.roll(centre, depth - 1, 1))
            lower = jnp.where(bottom, 0.0, pltpu.roll(centre, 1, 1))
            laps.append((east + west + north + south + upper + lower - 6.0 * centre, centre))
            steps_x.append(0.5 * (east - west))
            steps_y.append(0.5 * (north - south))
        for c in range(comps):
            flux = jac_ref[0, c, 0] * steps_x[0]
            for d in range(1, comps):
                flux = flux + jac_ref[0, c, d] * steps_x[d]
            for d in range(comps):
                flux = flux + jac_ref[1, c, d] * steps_y[d]
            lap, centre = laps[c]
            value = keep * centre + rate * (dif * lap - flux)
            if blend:
                value = value + blend * extra_ref[c, x]
            out_ref[c, x] = value
        return carry

    lax.fori_loop(0, rows, row, 0)


def apply_flux(padded, diffusivity, extra, jacobians, keep, blend, rate, interpret=False):
    out_shape = jax.ShapeDtypeStruct((padded.shape[0],) + diffusivity.shape, jnp.float32)
    vmem = pl.BlockSpec(memory_space=pltpu.VMEM)
    return pl.pallas_call(
        functools.partial(flux_kernel, keep=keep, blend=blend, rate=rate),
        out_shape=out_shape,
        in_specs=[pl.BlockSpec(memory_space=pltpu.SMEM), vmem, vmem, vmem],
        out_specs=vmem,
        interpret=interpret,
    )(jacobians, padded, diffusivity, extra)


def face_rim(field):
    return with_halo(field, (("sec", 1), ("blk", 2)), 1)


def plane_sides(plane):
    sides = []
    for axis, dim in (("sec", 1), ("blk", 2)):
        size, length = (lax.axis_size(axis), plane.shape[dim])
        up = [(i, i + 1) for i in range(size - 1)]
        down = [(j, i) for i, j in up]
        before = lax.ppermute(lax.slice_in_dim(plane, length - 1, length, axis=dim), axis, up)
        after = lax.ppermute(lax.slice_in_dim(plane, 0, 1, axis=dim), axis, down)
        ahead = jnp.concatenate([lax.slice_in_dim(plane, 1, length, axis=dim), after], axis=dim)
        behind = jnp.concatenate([before, lax.slice_in_dim(plane, 0, length - 1, axis=dim)], axis=dim)
        sides.append((ahead, behind))
    return sides


def local(
    fluid_state,
    diffusivity,
    first_jacobian,
    second_jacobian,
    wall_normal,
    interpolation,
    target_device,
    target_tile,
    live_tiles,
    displacement,
    stiff_diagonal,
    stiff_tiles,
    stiff_columns,
):
    devices = lax.axis_size(("sec", "blk"))
    wall_tiles = interpolation.shape[0]
    fan_tiles = interpolation.shape[1]
    tile_size = interpolation.shape[2]
    slots_each = 2 * wall_tiles * fan_tiles // devices
    total_slots = devices * slots_each
    pair_count = wall_tiles * fan_tiles
    shell_tiles = displacement.shape[1] // tile_size
    rows_first = fluid_state.shape[1]
    rows_second = fluid_state.shape[2]
    destination = target_device.reshape(pair_count)
    position = jnp.arange(pair_count, dtype=jnp.int32)
    earlier = (destination[:, None] == destination[None, :]) & (
        position[None, :] < position[:, None]
    )
    rank_within = jnp.sum(earlier.astype(jnp.int32), axis=1)
    slot_index = destination * slots_each + rank_within
    slot_match = slot_index[:, None] == jnp.arange(total_slots, dtype=jnp.int32)[None, :]
    slot_table = slot_match.astype(jnp.float32)
    tile_plus = target_tile.reshape(pair_count) + 1
    sent_tiles = jnp.sum(jnp.where(slot_match, tile_plus[:, None], 0), axis=0) - 1
    owned_tiles = lax.all_to_all(
        sent_tiles.reshape(devices, slots_each),
        ("sec", "blk"),
        split_axis=0,
        concat_axis=0,
        tiled=True,
    ).reshape(total_slots)
    owner_table = (
        owned_tiles[:, None] == jnp.arange(shell_tiles, dtype=jnp.int32)[None, :]
    ).astype(jnp.float32)
    live_mask = (jnp.arange(wall_tiles, dtype=jnp.int32) < live_tiles[0]).astype(jnp.float32)
    column_table = (
        stiff_columns[:, :, None] == jnp.arange(shell_tiles + 2, dtype=jnp.int32)[None, None, :]
    ).astype(jnp.float32)

    def send_forth(buffer):
        arrived = lax.all_to_all(buffer, ("sec", "blk"), split_axis=0, concat_axis=0, tiled=True)
        return arrived

    def shell_forces(wall_value):
        traction = wall_normal * wall_value[None]
        traction_tiles = traction.reshape(3, wall_tiles, tile_size)
        contribution = jnp.einsum(
            "rkqn,crq->rkcn", interpolation, traction_tiles, precision=HIGH
        )
        contribution = contribution * live_mask[:, None, None, None]
        outgoing = jnp.einsum(
            "pm,pcn->mcn",
            slot_table,
            contribution.reshape(pair_count, 3, tile_size),
            precision=HIGHEST,
        )
        arrived = send_forth(outgoing.reshape(devices, slots_each, 3, tile_size)).reshape(
            total_slots, 3, tile_size
        )
        forces = jnp.einsum("ms,mcn->csn", owner_table, arrived, precision=HIGHEST)
        return forces.reshape(3, shell_tiles * tile_size)

    def off_diagonal(values):
        window = with_halo(values, ((("sec", "blk"), 1),), tile_size)
        window_tiles = window.reshape(3, shell_tiles + 2, tile_size)
        chosen = jnp.einsum("ibj,cjn->ibcn", column_table, window_tiles, precision=HIGHEST)
        result = jnp.einsum("ibmn,ibcn->cim", stiff_tiles, chosen, precision=HIGH)
        return result.reshape(3, shell_tiles * tile_size)

    def shell_update(current, wall_value):
        forces = shell_forces(wall_value)
        estimate = current
        for sweep_index in range(SWEEPS):
            estimate = (forces - off_diagonal(estimate)) / stiff_diagonal
        return (1.0 - RELAXATION) * current + RELAXATION * estimate

    wall_bottom = diffusivity[:, :, 0]
    wall_above = diffusivity[:, :, 1]
    jacobians = jnp.stack([first_jacobian, second_jacobian])
    first_section = apply_flux(
        face_rim(fluid_state), diffusivity, fluid_state, jacobians, 1.0, 0.0, TIME_STEP
    )
    settled = apply_flux(
        face_rim(first_section), diffusivity, fluid_state, jacobians, 0.5, 0.5, 0.5 * TIME_STEP
    )
    settled = lax.optimization_barrier(settled)
    settled_wall = settled[4, :, :, 0]
    half_square = 0.5 * TIME_STEP * TIME_STEP
    edge_rows = jnp.array([1.0, 0.0, 0.0, 0.0, 1.0], jnp.float32)

    def wall_state(motion_plane):
        source = motion_plane * wall_bottom[None]
        (east_side, west_side), (north_side, south_side) = plane_sides(source)
        first_step = 0.5 * (east_side - west_side)
        second_step = 0.5 * (north_side - south_side)
        first_flux = jnp.stack([mixed(first_jacobian[:, 1:4], c, first_step) for c in range(5)])
        second_flux = jnp.stack([mixed(second_jacobian[:, 1:4], c, second_step) for c in range(5)])
        return source, east_side + west_side + north_side + south_side, first_flux, second_flux

    current = displacement
    for iteration in range(ITERS):
        shell_blocks = current.reshape(3, shell_tiles, tile_size)
        reply_tiles = jnp.einsum("ms,csn->mcn", owner_table, shell_blocks, precision=HIGHEST)
        returned = lax.all_to_all(
            reply_tiles.reshape(devices, slots_each, 3, tile_size),
            ("sec", "blk"),
            split_axis=0,
            concat_axis=0,
            tiled=True,
        )
        interface_returned = returned.reshape(total_slots, 3, tile_size)
        pair_values = jnp.einsum("pm,mcn->pcn", slot_table, interface_returned, precision=HIGHEST)
        pair_values = pair_values.reshape(wall_tiles, fan_tiles, 3, tile_size)
        motion = (
            jnp.einsum("rkqn,rkcn->rcq", interpolation, pair_values, precision=HIGH)
            * live_mask[:, None, None]
        )
        motion_plane = motion.transpose(1, 0, 2).reshape(3, rows_first, rows_second)
        source, neighbours, first_flux, second_flux = wall_state(motion_plane)
        wall_value = settled_wall - half_square * (first_flux[4] + second_flux[4])
        current = shell_update(current, wall_value)
    bottom = TIME_STEP * source + half_square * (
        wall_bottom[None] * (neighbours - 6.0 * source) - first_flux[1:4] - second_flux[1:4]
    )
    above = half_square * wall_above[None] * source
    zero_plane = jnp.zeros_like(source[:1])
    bottom = jnp.concatenate([zero_plane, bottom, zero_plane], axis=0)
    bottom = bottom - half_square * (first_flux + second_flux) * edge_rows[:, None, None]
    above = jnp.concatenate([zero_plane, above, zero_plane], axis=0)
    depth = lax.broadcasted_iota(jnp.int32, settled.shape, 3)
    fluid_field = settled + jnp.where(
        depth == 0, bottom[..., None], jnp.where(depth == 1, above[..., None], 0.0)
    )
    return (fluid_field, current)


def solution(mesh):
    return jax.shard_map(
        local,
        mesh=mesh,
        in_specs=(
            P(None, "sec", "blk", None),
            P("sec", "blk", None),
            P(),
            P(),
            P(None, "sec", "blk"),
            P(("sec", "blk"), None, None, None),
            P(("sec", "blk"), None),
            P(("sec", "blk"), None),
            P(("sec", "blk")),
            P(None, ("sec", "blk")),
            P(None, ("sec", "blk")),
            P(("sec", "blk"), None, None, None),
            P(("sec", "blk"), None),
        ),
        out_specs=(P(None, "sec", "blk", None), P(None, ("sec", "blk"))),
        check_vma=False,
    )
```

```python
import functools

import jax
import jax.numpy as jnp
from jax import lax
from jax.experimental import pallas as pl
from jax.experimental.pallas import tpu as pltpu
from jax.sharding import PartitionSpec as P

ITERS = 3
SWEEPS = 3


TIME_STEP = 0.04
RELAXATION = 0.5
HIGHEST = lax.Precision.HIGHEST
HIGH = lax.Precision.HIGH


def with_halo(array, sides, width):
    for axis, dim in sides:
        size, length = (lax.axis_size(axis), array.shape[dim])
        up = [(i, (i + 1) % size) for i in range(size - 1)]
        down = [(j, i) for i, j in up]
        last = lax.slice_in_dim(array, length - width, length, axis=dim)
        first = lax.slice_in_dim(array, 0, width, axis=dim)
        before = lax.ppermute(last, axis, up)
        after = lax.ppermute(first, axis, down)
        array = jnp.concatenate([before, array, after], axis=dim)
    return array


def homogeneous(padded, diffusivity, first_jacobian, second_jacobian):
    centre = padded[:, 1:-1, 1:-1]
    east_side = padded[:, 2:, 1:-1]
    west_side = padded[:, :-2, 1:-1]
    north_side = padded[:, 1:-1, 2:]
    south_side = padded[:, 1:-1, :-2]
    zero_layer = jnp.zeros(centre.shape[:-1] + (1,), jnp.float32)
    upper_side = jnp.concatenate([centre[..., 1:], zero_layer], axis=3)
    lower_side = jnp.concatenate([zero_layer, centre[..., :-1]], axis=3)
    laplace = (
        east_side + west_side + north_side + south_side + upper_side + lower_side - 6.0 * centre
    )
    first_flux = jnp.einsum(
        "cd,dxyz->cxyz", first_jacobian, 0.5 * (east_side - west_side), precision=HIGH
    )
    second_flux = jnp.einsum(
        "cd,dxyz->cxyz", second_jacobian, 0.5 * (north_side - south_side), precision=HIGH
    )
    return diffusivity[None] * laplace - first_flux - second_flux


def mixed(jacobian, row, values):
    total = jacobian[row, 0] * values[0]
    for d in range(1, values.shape[0]):
        total = total + jacobian[row, d] * values[d]
    return total


def flux_kernel(jac_ref, pad_ref, dif_ref, extra_ref, out_ref, *, keep, blend, rate):
    comps, rows, cols, depth = out_ref.shape
    lanes = lax.broadcasted_iota(jnp.int32, (cols, depth), 1)
    top = lanes == depth - 1
    bottom = lanes == 0

    def row(x, carry):
        dif = dif_ref[x]
        steps_x, steps_y, laps = [], [], []
        for d in range(comps):
            east = pad_ref[d, x + 2, pl.ds(1, cols), :]
            west = pad_ref[d, x, pl.ds(1, cols), :]
            north = pad_ref[d, x + 1, pl.ds(2, cols), :]
            south = pad_ref[d, x + 1, pl.ds(0, cols), :]
            centre = pad_ref[d, x + 1, pl.ds(1, cols), :]
            upper = jnp.where(top, 0.0, pltpu.roll(centre, depth - 1, 1))
            lower = jnp.where(bottom, 0.0, pltpu.roll(centre, 1, 1))
            laps.append((east + west + north + south + upper + lower - 6.0 * centre, centre))
            steps_x.append(0.5 * (east - west))
            steps_y.append(0.5 * (north - south))
        for c in range(comps):
            flux = jac_ref[0, c, 0] * steps_x[0]
            for d in range(1, comps):
                flux = flux + jac_ref[0, c, d] * steps_x[d]
            for d in range(comps):
                flux = flux + jac_ref[1, c, d] * steps_y[d]
            lap, centre = laps[c]
            value = keep * centre + rate * (dif * lap - flux)
            if blend:
                value = value + blend * extra_ref[c, x]
            out_ref[c, x] = value
        return carry

    lax.fori_loop(0, rows, row, 0, unroll=2)


def apply_flux(padded, diffusivity, extra, jacobians, keep, blend, rate, interpret=False):
    out_shape = jax.ShapeDtypeStruct((padded.shape[0],) + diffusivity.shape, jnp.float32)
    vmem = pl.BlockSpec(memory_space=pltpu.VMEM)
    return pl.pallas_call(
        functools.partial(flux_kernel, keep=keep, blend=blend, rate=rate),
        out_shape=out_shape,
        in_specs=[pl.BlockSpec(memory_space=pltpu.SMEM), vmem, vmem, vmem],
        out_specs=vmem,
        interpret=interpret,
    )(jacobians, padded, diffusivity, extra)


def face_rim(field):
    pieces = {}
    for axis, dim in (("sec", 1), ("blk", 2)):
        size, length = (lax.axis_size(axis), field.shape[dim])
        up = [(i, i + 1) for i in range(size - 1)]
        down = [(j, i) for i, j in up]
        before = lax.ppermute(lax.slice_in_dim(field, length - 1, length, axis=dim), axis, up)
        after = lax.ppermute(lax.slice_in_dim(field, 0, 1, axis=dim), axis, down)
        pieces[dim] = (before, after)
    middle = jnp.concatenate([pieces[2][0], field, pieces[2][1]], axis=2)
    corner = jnp.zeros(field.shape[:1] + (1, 1) + field.shape[3:], field.dtype)
    before_x, after_x = (jnp.concatenate([corner, edge, corner], axis=2) for edge in pieces[1])
    return jnp.concatenate([before_x, middle, after_x], axis=1)


def plane_sides(plane):
    sides = []
    for axis, dim in (("sec", 1), ("blk", 2)):
        size, length = (lax.axis_size(axis), plane.shape[dim])
        up = [(i, i + 1) for i in range(size - 1)]
        down = [(j, i) for i, j in up]
        before = lax.ppermute(lax.slice_in_dim(plane, length - 1, length, axis=dim), axis, up)
        after = lax.ppermute(lax.slice_in_dim(plane, 0, 1, axis=dim), axis, down)
        ahead = jnp.concatenate([lax.slice_in_dim(plane, 1, length, axis=dim), after], axis=dim)
        behind = jnp.concatenate([before, lax.slice_in_dim(plane, 0, length - 1, axis=dim)], axis=dim)
        sides.append((ahead, behind))
    return sides


def local(
    fluid_state,
    diffusivity,
    first_jacobian,
    second_jacobian,
    wall_normal,
    interpolation,
    target_device,
    target_tile,
    live_tiles,
    displacement,
    stiff_diagonal,
    stiff_tiles,
    stiff_columns,
):
    devices = lax.axis_size(("sec", "blk"))
    wall_tiles = interpolation.shape[0]
    fan_tiles = interpolation.shape[1]
    tile_size = interpolation.shape[2]
    slots_each = 2 * wall_tiles * fan_tiles // devices
    total_slots = devices * slots_each
    pair_count = wall_tiles * fan_tiles
    shell_tiles = displacement.shape[1] // tile_size
    rows_first = fluid_state.shape[1]
    rows_second = fluid_state.shape[2]
    destination = target_device.reshape(pair_count)
    position = jnp.arange(pair_count, dtype=jnp.int32)
    earlier = (destination[:, None] == destination[None, :]) & (
        position[None, :] < position[:, None]
    )
    rank_within = jnp.sum(earlier.astype(jnp.int32), axis=1)
    slot_index = destination * slots_each + rank_within
    slot_match = slot_index[:, None] == jnp.arange(total_slots, dtype=jnp.int32)[None, :]
    slot_table = slot_match.astype(jnp.float32)
    tile_plus = target_tile.reshape(pair_count) + 1
    sent_tiles = jnp.sum(jnp.where(slot_match, tile_plus[:, None], 0), axis=0) - 1
    owned_tiles = lax.all_to_all(
        sent_tiles.reshape(devices, slots_each),
        ("sec", "blk"),
        split_axis=0,
        concat_axis=0,
        tiled=True,
    ).reshape(total_slots)
    owner_table = (
        owned_tiles[:, None] == jnp.arange(shell_tiles, dtype=jnp.int32)[None, :]
    ).astype(jnp.float32)
    live_mask = (jnp.arange(wall_tiles, dtype=jnp.int32) < live_tiles[0]).astype(jnp.float32)
    column_table = (
        stiff_columns[:, :, None] == jnp.arange(shell_tiles + 2, dtype=jnp.int32)[None, None, :]
    ).astype(jnp.float32)

    def send_forth(buffer):
        arrived = lax.all_to_all(buffer, ("sec", "blk"), split_axis=0, concat_axis=0, tiled=True)
        return arrived

    def shell_forces(wall_value):
        traction = wall_normal * wall_value[None]
        traction_tiles = traction.reshape(3, wall_tiles, tile_size)
        contribution = jnp.einsum(
            "rkqn,crq->rkcn", interpolation, traction_tiles, precision=HIGH
        )
        contribution = contribution * live_mask[:, None, None, None]
        outgoing = jnp.einsum(
            "pm,pcn->mcn",
            slot_table,
            contribution.reshape(pair_count, 3, tile_size),
            precision=HIGHEST,
        )
        arrived = send_forth(outgoing.reshape(devices, slots_each, 3, tile_size)).reshape(
            total_slots, 3, tile_size
        )
        forces = jnp.einsum("ms,mcn->csn", owner_table, arrived, precision=HIGHEST)
        return forces.reshape(3, shell_tiles * tile_size)

    def off_diagonal(values):
        window = with_halo(values, ((("sec", "blk"), 1),), tile_size)
        window_tiles = window.reshape(3, shell_tiles + 2, tile_size)
        chosen = jnp.einsum("ibj,cjn->ibcn", column_table, window_tiles, precision=HIGHEST)
        result = jnp.einsum("ibmn,ibcn->cim", stiff_tiles, chosen, precision=HIGH)
        return result.reshape(3, shell_tiles * tile_size)

    def shell_update(current, wall_value):
        forces = shell_forces(wall_value)
        estimate = current
        for sweep_index in range(SWEEPS):
            estimate = (forces - off_diagonal(estimate)) / stiff_diagonal
        return (1.0 - RELAXATION) * current + RELAXATION * estimate

    wall_bottom = diffusivity[:, :, 0]
    wall_above = diffusivity[:, :, 1]
    jacobians = jnp.stack([first_jacobian, second_jacobian])
    first_section = apply_flux(
        face_rim(fluid_state), diffusivity, fluid_state, jacobians, 1.0, 0.0, TIME_STEP
    )
    settled = apply_flux(
        face_rim(first_section), diffusivity, fluid_state, jacobians, 0.5, 0.5, 0.5 * TIME_STEP
    )
    settled = lax.optimization_barrier(settled)
    settled_wall = settled[4, :, :, 0]
    half_square = 0.5 * TIME_STEP * TIME_STEP
    edge_rows = jnp.array([1.0, 0.0, 0.0, 0.0, 1.0], jnp.float32)

    def wall_state(motion_plane):
        source = motion_plane * wall_bottom[None]
        (east_side, west_side), (north_side, south_side) = plane_sides(source)
        first_step = 0.5 * (east_side - west_side)
        second_step = 0.5 * (north_side - south_side)
        first_flux = jnp.stack([mixed(first_jacobian[:, 1:4], c, first_step) for c in range(5)])
        second_flux = jnp.stack([mixed(second_jacobian[:, 1:4], c, second_step) for c in range(5)])
        return source, east_side + west_side + north_side + south_side, first_flux, second_flux

    current = displacement
    for iteration in range(ITERS):
        shell_blocks = current.reshape(3, shell_tiles, tile_size)
        reply_tiles = jnp.einsum("ms,csn->mcn", owner_table, shell_blocks, precision=HIGHEST)
        returned = lax.all_to_all(
            reply_tiles.reshape(devices, slots_each, 3, tile_size),
            ("sec", "blk"),
            split_axis=0,
            concat_axis=0,
            tiled=True,
        )
        interface_returned = returned.reshape(total_slots, 3, tile_size)
        pair_values = jnp.einsum("pm,mcn->pcn", slot_table, interface_returned, precision=HIGHEST)
        pair_values = pair_values.reshape(wall_tiles, fan_tiles, 3, tile_size)
        motion = (
            jnp.einsum("rkqn,rkcn->rcq", interpolation, pair_values, precision=HIGH)
            * live_mask[:, None, None]
        )
        motion_plane = motion.transpose(1, 0, 2).reshape(3, rows_first, rows_second)
        source, neighbours, first_flux, second_flux = wall_state(motion_plane)
        wall_value = settled_wall - half_square * (first_flux[4] + second_flux[4])
        current = shell_update(current, wall_value)
    bottom = TIME_STEP * source + half_square * (
        wall_bottom[None] * (neighbours - 6.0 * source) - first_flux[1:4] - second_flux[1:4]
    )
    above = half_square * wall_above[None] * source
    zero_plane = jnp.zeros_like(source[:1])
    bottom = jnp.concatenate([zero_plane, bottom, zero_plane], axis=0)
    bottom = bottom - half_square * (first_flux + second_flux) * edge_rows[:, None, None]
    above = jnp.concatenate([zero_plane, above, zero_plane], axis=0)
    depth = lax.broadcasted_iota(jnp.int32, settled.shape, 3)
    fluid_field = settled + jnp.where(
        depth == 0, bottom[..., None], jnp.where(depth == 1, above[..., None], 0.0)
    )
    return (fluid_field, current)


def solution(mesh):
    return jax.shard_map(
        local,
        mesh=mesh,
        in_specs=(
            P(None, "sec", "blk", None),
            P("sec", "blk", None),
            P(),
            P(),
            P(None, "sec", "blk"),
            P(("sec", "blk"), None, None, None),
            P(("sec", "blk"), None),
            P(("sec", "blk"), None),
            P(("sec", "blk")),
            P(None, ("sec", "blk")),
            P(None, ("sec", "blk")),
            P(("sec", "blk"), None, None, None),
            P(("sec", "blk"), None),
        ),
        out_specs=(P(None, "sec", "blk", None), P(None, ("sec", "blk"))),
        check_vma=False,
    )
```

```python
import functools

import jax
import jax.numpy as jnp
from jax import lax
from jax.experimental import pallas as pl
from jax.experimental.pallas import tpu as pltpu
from jax.sharding import PartitionSpec as P

ITERS = 3
SWEEPS = 3


TIME_STEP = 0.04
RELAXATION = 0.5
HIGHEST = lax.Precision.HIGHEST
HIGH = lax.Precision.HIGH


def with_halo(array, sides, width):
    for axis, dim in sides:
        size, length = (lax.axis_size(axis), array.shape[dim])
        up = [(i, (i + 1) % size) for i in range(size - 1)]
        down = [(j, i) for i, j in up]
        last = lax.slice_in_dim(array, length - width, length, axis=dim)
        first = lax.slice_in_dim(array, 0, width, axis=dim)
        before = lax.ppermute(last, axis, up)
        after = lax.ppermute(first, axis, down)
        array = jnp.concatenate([before, array, after], axis=dim)
    return array


def homogeneous(padded, diffusivity, first_jacobian, second_jacobian):
    centre = padded[:, 1:-1, 1:-1]
    east_side = padded[:, 2:, 1:-1]
    west_side = padded[:, :-2, 1:-1]
    north_side = padded[:, 1:-1, 2:]
    south_side = padded[:, 1:-1, :-2]
    zero_layer = jnp.zeros(centre.shape[:-1] + (1,), jnp.float32)
    upper_side = jnp.concatenate([centre[..., 1:], zero_layer], axis=3)
    lower_side = jnp.concatenate([zero_layer, centre[..., :-1]], axis=3)
    laplace = (
        east_side + west_side + north_side + south_side + upper_side + lower_side - 6.0 * centre
    )
    first_flux = jnp.einsum(
        "cd,dxyz->cxyz", first_jacobian, 0.5 * (east_side - west_side), precision=HIGH
    )
    second_flux = jnp.einsum(
        "cd,dxyz->cxyz", second_jacobian, 0.5 * (north_side - south_side), precision=HIGH
    )
    return diffusivity[None] * laplace - first_flux - second_flux


def flat_blend(jacobian, values):
    total = jacobian[:, 0, None, None] * values[0][None]
    for d in range(1, values.shape[0]):
        total = total + jacobian[:, d, None, None] * values[d][None]
    return total


def mixed(jacobian, row, values):
    total = jacobian[row, 0] * values[0]
    for d in range(1, values.shape[0]):
        total = total + jacobian[row, d] * values[d]
    return total


def flux_kernel(jac_ref, pad_ref, dif_ref, extra_ref, out_ref, *, keep, blend, rate):
    comps, rows, cols, depth = out_ref.shape
    lanes = lax.broadcasted_iota(jnp.int32, (cols, depth), 1)
    top = lanes == depth - 1
    bottom = lanes == 0

    def row(x, carry):
        dif = dif_ref[x]
        steps_x, steps_y, laps = [], [], []
        for d in range(comps):
            east = pad_ref[d, x + 2, pl.ds(1, cols), :]
            west = pad_ref[d, x, pl.ds(1, cols), :]
            north = pad_ref[d, x + 1, pl.ds(2, cols), :]
            south = pad_ref[d, x + 1, pl.ds(0, cols), :]
            centre = pad_ref[d, x + 1, pl.ds(1, cols), :]
            upper = jnp.where(top, 0.0, pltpu.roll(centre, depth - 1, 1))
            lower = jnp.where(bottom, 0.0, pltpu.roll(centre, 1, 1))
            laps.append((east + west + north + south + upper + lower - 6.0 * centre, centre))
            steps_x.append(0.5 * (east - west))
            steps_y.append(0.5 * (north - south))
        for c in range(comps):
            flux = jac_ref[0, c, 0] * steps_x[0]
            for d in range(1, comps):
                flux = flux + jac_ref[0, c, d] * steps_x[d]
            for d in range(comps):
                flux = flux + jac_ref[1, c, d] * steps_y[d]
            lap, centre = laps[c]
            value = keep * centre + rate * (dif * lap - flux)
            if blend:
                value = value + blend * extra_ref[c, x]
            out_ref[c, x] = value
        return carry

    lax.fori_loop(0, rows, row, 0, unroll=2)


def apply_flux(padded, diffusivity, extra, jacobians, keep, blend, rate, interpret=False):
    out_shape = jax.ShapeDtypeStruct((padded.shape[0],) + diffusivity.shape, jnp.float32)
    vmem = pl.BlockSpec(memory_space=pltpu.VMEM)
    return pl.pallas_call(
        functools.partial(flux_kernel, keep=keep, blend=blend, rate=rate),
        out_shape=out_shape,
        in_specs=[pl.BlockSpec(memory_space=pltpu.SMEM), vmem, vmem, vmem],
        out_specs=vmem,
        interpret=interpret,
    )(jacobians, padded, diffusivity, extra)


def face_rim(field):
    pieces = {}
    for axis, dim in (("sec", 1), ("blk", 2)):
        size, length = (lax.axis_size(axis), field.shape[dim])
        up = [(i, i + 1) for i in range(size - 1)]
        down = [(j, i) for i, j in up]
        before = lax.ppermute(lax.slice_in_dim(field, length - 1, length, axis=dim), axis, up)
        after = lax.ppermute(lax.slice_in_dim(field, 0, 1, axis=dim), axis, down)
        pieces[dim] = (before, after)
    middle = jnp.concatenate([pieces[2][0], field, pieces[2][1]], axis=2)
    corner = jnp.zeros(field.shape[:1] + (1, 1) + field.shape[3:], field.dtype)
    before_x, after_x = (jnp.concatenate([corner, edge, corner], axis=2) for edge in pieces[1])
    return jnp.concatenate([before_x, middle, after_x], axis=1)


def plane_sides(plane):
    sides = []
    for axis, dim in (("sec", 1), ("blk", 2)):
        size, length = (lax.axis_size(axis), plane.shape[dim])
        up = [(i, i + 1) for i in range(size - 1)]
        down = [(j, i) for i, j in up]
        before = lax.ppermute(lax.slice_in_dim(plane, length - 1, length, axis=dim), axis, up)
        after = lax.ppermute(lax.slice_in_dim(plane, 0, 1, axis=dim), axis, down)
        ahead = jnp.concatenate([lax.slice_in_dim(plane, 1, length, axis=dim), after], axis=dim)
        behind = jnp.concatenate([before, lax.slice_in_dim(plane, 0, length - 1, axis=dim)], axis=dim)
        sides.append((ahead, behind))
    return sides


def local(
    fluid_state,
    diffusivity,
    first_jacobian,
    second_jacobian,
    wall_normal,
    interpolation,
    target_device,
    target_tile,
    live_tiles,
    displacement,
    stiff_diagonal,
    stiff_tiles,
    stiff_columns,
):
    devices = lax.axis_size(("sec", "blk"))
    wall_tiles = interpolation.shape[0]
    fan_tiles = interpolation.shape[1]
    tile_size = interpolation.shape[2]
    slots_each = 2 * wall_tiles * fan_tiles // devices
    total_slots = devices * slots_each
    pair_count = wall_tiles * fan_tiles
    shell_tiles = displacement.shape[1] // tile_size
    rows_first = fluid_state.shape[1]
    rows_second = fluid_state.shape[2]
    destination = target_device.reshape(pair_count)
    position = jnp.arange(pair_count, dtype=jnp.int32)
    earlier = (destination[:, None] == destination[None, :]) & (
        position[None, :] < position[:, None]
    )
    rank_within = jnp.sum(earlier.astype(jnp.int32), axis=1)
    slot_index = destination * slots_each + rank_within
    slot_match = slot_index[:, None] == jnp.arange(total_slots, dtype=jnp.int32)[None, :]
    slot_table = slot_match.astype(jnp.float32)
    tile_plus = target_tile.reshape(pair_count) + 1
    sent_tiles = jnp.sum(jnp.where(slot_match, tile_plus[:, None], 0), axis=0) - 1
    owned_tiles = lax.all_to_all(
        sent_tiles.reshape(devices, slots_each),
        ("sec", "blk"),
        split_axis=0,
        concat_axis=0,
        tiled=True,
    ).reshape(total_slots)
    owner_table = (
        owned_tiles[:, None] == jnp.arange(shell_tiles, dtype=jnp.int32)[None, :]
    ).astype(jnp.float32)
    live_mask = (jnp.arange(wall_tiles, dtype=jnp.int32) < live_tiles[0]).astype(jnp.float32)
    column_table = (
        stiff_columns[:, :, None] == jnp.arange(shell_tiles + 2, dtype=jnp.int32)[None, None, :]
    ).astype(jnp.float32)

    def send_forth(buffer):
        arrived = lax.all_to_all(buffer, ("sec", "blk"), split_axis=0, concat_axis=0, tiled=True)
        return arrived

    def shell_forces(wall_value):
        traction = wall_normal * wall_value[None]
        traction_tiles = traction.reshape(3, wall_tiles, tile_size)
        contribution = jnp.einsum(
            "rkqn,crq->rkcn", interpolation, traction_tiles, precision=HIGH
        )
        contribution = contribution * live_mask[:, None, None, None]
        outgoing = jnp.einsum(
            "pm,pcn->mcn",
            slot_table,
            contribution.reshape(pair_count, 3, tile_size),
            precision=HIGHEST,
        )
        arrived = send_forth(outgoing.reshape(devices, slots_each, 3, tile_size)).reshape(
            total_slots, 3, tile_size
        )
        forces = jnp.einsum("ms,mcn->csn", owner_table, arrived, precision=HIGHEST)
        return forces.reshape(3, shell_tiles * tile_size)

    def off_diagonal(values):
        window = with_halo(values, ((("sec", "blk"), 1),), tile_size)
        window_tiles = window.reshape(3, shell_tiles + 2, tile_size)
        chosen = jnp.einsum("ibj,cjn->ibcn", column_table, window_tiles, precision=HIGHEST)
        result = jnp.einsum("ibmn,ibcn->cim", stiff_tiles, chosen, precision=HIGH)
        return result.reshape(3, shell_tiles * tile_size)

    def shell_update(current, wall_value):
        forces = shell_forces(wall_value)
        estimate = current
        for sweep_index in range(SWEEPS):
            estimate = (forces - off_diagonal(estimate)) / stiff_diagonal
        return (1.0 - RELAXATION) * current + RELAXATION * estimate

    wall_bottom = diffusivity[:, :, 0]
    wall_above = diffusivity[:, :, 1]
    jacobians = jnp.stack([first_jacobian, second_jacobian])
    first_section = apply_flux(
        face_rim(fluid_state), diffusivity, fluid_state, jacobians, 1.0, 0.0, TIME_STEP
    )
    settled = apply_flux(
        face_rim(first_section), diffusivity, fluid_state, jacobians, 0.5, 0.5, 0.5 * TIME_STEP
    )
    settled = lax.optimization_barrier(settled)
    settled_wall = settled[4, :, :, 0]
    half_square = 0.5 * TIME_STEP * TIME_STEP
    edge_rows = jnp.array([1.0, 0.0, 0.0, 0.0, 1.0], jnp.float32)

    def wall_state(motion_plane):
        source = motion_plane * wall_bottom[None]
        (east_side, west_side), (north_side, south_side) = plane_sides(source)
        first_step = 0.5 * (east_side - west_side)
        second_step = 0.5 * (north_side - south_side)
        first_flux = flat_blend(first_jacobian[:, 1:4], first_step)
        second_flux = flat_blend(second_jacobian[:, 1:4], second_step)
        return source, east_side + west_side + north_side + south_side, first_flux, second_flux

    current = displacement
    for iteration in range(ITERS):
        shell_blocks = current.reshape(3, shell_tiles, tile_size)
        reply_tiles = jnp.einsum("ms,csn->mcn", owner_table, shell_blocks, precision=HIGHEST)
        returned = lax.all_to_all(
            reply_tiles.reshape(devices, slots_each, 3, tile_size),
            ("sec", "blk"),
            split_axis=0,
            concat_axis=0,
            tiled=True,
        )
        interface_returned = returned.reshape(total_slots, 3, tile_size)
        pair_values = jnp.einsum("pm,mcn->pcn", slot_table, interface_returned, precision=HIGHEST)
        pair_values = pair_values.reshape(wall_tiles, fan_tiles, 3, tile_size)
        motion = (
            jnp.einsum("rkqn,rkcn->rcq", interpolation, pair_values, precision=HIGH)
            * live_mask[:, None, None]
        )
        motion_plane = motion.transpose(1, 0, 2).reshape(3, rows_first, rows_second)
        source, neighbours, first_flux, second_flux = wall_state(motion_plane)
        wall_value = settled_wall - half_square * (first_flux[4] + second_flux[4])
        current = shell_update(current, wall_value)
    bottom = TIME_STEP * source + half_square * (
        wall_bottom[None] * (neighbours - 6.0 * source) - first_flux[1:4] - second_flux[1:4]
    )
    above = half_square * wall_above[None] * source
    zero_plane = jnp.zeros_like(source[:1])
    bottom = jnp.concatenate([zero_plane, bottom, zero_plane], axis=0)
    bottom = bottom - half_square * (first_flux + second_flux) * edge_rows[:, None, None]
    above = jnp.concatenate([zero_plane, above, zero_plane], axis=0)
    depth = lax.broadcasted_iota(jnp.int32, settled.shape, 3)
    fluid_field = settled + jnp.where(
        depth == 0, bottom[..., None], jnp.where(depth == 1, above[..., None], 0.0)
    )
    return (fluid_field, current)


def solution(mesh):
    return jax.shard_map(
        local,
        mesh=mesh,
        in_specs=(
            P(None, "sec", "blk", None),
            P("sec", "blk", None),
            P(),
            P(),
            P(None, "sec", "blk"),
            P(("sec", "blk"), None, None, None),
            P(("sec", "blk"), None),
            P(("sec", "blk"), None),
            P(("sec", "blk")),
            P(None, ("sec", "blk")),
            P(None, ("sec", "blk")),
            P(("sec", "blk"), None, None, None),
            P(("sec", "blk"), None),
        ),
        out_specs=(P(None, "sec", "blk", None), P(None, ("sec", "blk"))),
        check_vma=False,
    )
```

```python
import functools

import jax
import jax.numpy as jnp
from jax import lax
from jax.experimental import pallas as pl
from jax.experimental.pallas import tpu as pltpu
from jax.sharding import PartitionSpec as P

ITERS = 3
SWEEPS = 3


TIME_STEP = 0.04
RELAXATION = 0.5
HIGHEST = lax.Precision.HIGHEST
HIGH = lax.Precision.HIGH


def with_halo(array, sides, width):
    for axis, dim in sides:
        size, length = (lax.axis_size(axis), array.shape[dim])
        up = [(i, (i + 1) % size) for i in range(size - 1)]
        down = [(j, i) for i, j in up]
        last = lax.slice_in_dim(array, length - width, length, axis=dim)
        first = lax.slice_in_dim(array, 0, width, axis=dim)
        before = lax.ppermute(last, axis, up)
        after = lax.ppermute(first, axis, down)
        array = jnp.concatenate([before, array, after], axis=dim)
    return array


def homogeneous(padded, diffusivity, first_jacobian, second_jacobian):
    centre = padded[:, 1:-1, 1:-1]
    east_side = padded[:, 2:, 1:-1]
    west_side = padded[:, :-2, 1:-1]
    north_side = padded[:, 1:-1, 2:]
    south_side = padded[:, 1:-1, :-2]
    zero_layer = jnp.zeros(centre.shape[:-1] + (1,), jnp.float32)
    upper_side = jnp.concatenate([centre[..., 1:], zero_layer], axis=3)
    lower_side = jnp.concatenate([zero_layer, centre[..., :-1]], axis=3)
    laplace = (
        east_side + west_side + north_side + south_side + upper_side + lower_side - 6.0 * centre
    )
    first_flux = jnp.einsum(
        "cd,dxyz->cxyz", first_jacobian, 0.5 * (east_side - west_side), precision=HIGH
    )
    second_flux = jnp.einsum(
        "cd,dxyz->cxyz", second_jacobian, 0.5 * (north_side - south_side), precision=HIGH
    )
    return diffusivity[None] * laplace - first_flux - second_flux


def flat_blend(jacobian, values):
    total = jacobian[:, 0, None, None] * values[0][None]
    for d in range(1, values.shape[0]):
        total = total + jacobian[:, d, None, None] * values[d][None]
    return total


def mixed(jacobian, row, values):
    total = jacobian[row, 0] * values[0]
    for d in range(1, values.shape[0]):
        total = total + jacobian[row, d] * values[d]
    return total


def flux_kernel(jac_ref, pad_ref, dif_ref, extra_ref, out_ref, *, keep, blend, rate):
    comps, rows, cols, depth = out_ref.shape
    lanes = lax.broadcasted_iota(jnp.int32, (cols, depth), 1)
    top = lanes == depth - 1
    bottom = lanes == 0

    def row(x, carry):
        dif = dif_ref[x]
        steps_x, steps_y, laps = [], [], []
        for d in range(comps):
            east = pad_ref[d, x + 2, pl.ds(1, cols), :]
            west = pad_ref[d, x, pl.ds(1, cols), :]
            north = pad_ref[d, x + 1, pl.ds(2, cols), :]
            south = pad_ref[d, x + 1, pl.ds(0, cols), :]
            centre = pad_ref[d, x + 1, pl.ds(1, cols), :]
            upper = jnp.where(top, 0.0, pltpu.roll(centre, depth - 1, 1))
            lower = jnp.where(bottom, 0.0, pltpu.roll(centre, 1, 1))
            laps.append((east + west + north + south + upper + lower - 6.0 * centre, centre))
            steps_x.append(0.5 * (east - west))
            steps_y.append(0.5 * (north - south))
        for c in range(comps):
            flux = jac_ref[0, c, 0] * steps_x[0]
            for d in range(1, comps):
                flux = flux + jac_ref[0, c, d] * steps_x[d]
            for d in range(comps):
                flux = flux + jac_ref[1, c, d] * steps_y[d]
            lap, centre = laps[c]
            value = keep * centre + rate * (dif * lap - flux)
            if blend:
                value = value + blend * extra_ref[c, x]
            out_ref[c, x] = value
        return carry

    lax.fori_loop(0, rows, row, 0, unroll=2)


def apply_flux(padded, diffusivity, extra, jacobians, keep, blend, rate, interpret=False):
    out_shape = jax.ShapeDtypeStruct((padded.shape[0],) + diffusivity.shape, jnp.float32)
    vmem = pl.BlockSpec(memory_space=pltpu.VMEM)
    return pl.pallas_call(
        functools.partial(flux_kernel, keep=keep, blend=blend, rate=rate),
        out_shape=out_shape,
        in_specs=[pl.BlockSpec(memory_space=pltpu.SMEM), vmem, vmem, vmem],
        out_specs=vmem,
        interpret=interpret,
    )(jacobians, padded, diffusivity, extra)


def face_rim(field):
    pieces = {}
    for axis, dim in (("sec", 1), ("blk", 2)):
        size, length = (lax.axis_size(axis), field.shape[dim])
        up = [(i, i + 1) for i in range(size - 1)]
        down = [(j, i) for i, j in up]
        before = lax.ppermute(lax.slice_in_dim(field, length - 1, length, axis=dim), axis, up)
        after = lax.ppermute(lax.slice_in_dim(field, 0, 1, axis=dim), axis, down)
        pieces[dim] = (before, after)
    middle = jnp.concatenate([pieces[2][0], field, pieces[2][1]], axis=2)
    corner = jnp.zeros(field.shape[:1] + (1, 1) + field.shape[3:], field.dtype)
    before_x, after_x = (jnp.concatenate([corner, edge, corner], axis=2) for edge in pieces[1])
    return jnp.concatenate([before_x, middle, after_x], axis=1)


def plane_sides(plane):
    sides = []
    for axis, dim in (("sec", 1), ("blk", 2)):
        size, length = (lax.axis_size(axis), plane.shape[dim])
        up = [(i, i + 1) for i in range(size - 1)]
        down = [(j, i) for i, j in up]
        before = lax.ppermute(lax.slice_in_dim(plane, length - 1, length, axis=dim), axis, up)
        after = lax.ppermute(lax.slice_in_dim(plane, 0, 1, axis=dim), axis, down)
        ahead = jnp.concatenate([lax.slice_in_dim(plane, 1, length, axis=dim), after], axis=dim)
        behind = jnp.concatenate([before, lax.slice_in_dim(plane, 0, length - 1, axis=dim)], axis=dim)
        sides.append((ahead, behind))
    return sides


def local(
    fluid_state,
    diffusivity,
    first_jacobian,
    second_jacobian,
    wall_normal,
    interpolation,
    target_device,
    target_tile,
    live_tiles,
    displacement,
    stiff_diagonal,
    stiff_tiles,
    stiff_columns,
):
    devices = lax.axis_size(("sec", "blk"))
    wall_tiles = interpolation.shape[0]
    fan_tiles = interpolation.shape[1]
    tile_size = interpolation.shape[2]
    slots_each = 2 * wall_tiles * fan_tiles // devices
    total_slots = devices * slots_each
    pair_count = wall_tiles * fan_tiles
    shell_tiles = displacement.shape[1] // tile_size
    rows_first = fluid_state.shape[1]
    rows_second = fluid_state.shape[2]
    destination = target_device.reshape(pair_count)
    position = jnp.arange(pair_count, dtype=jnp.int32)
    earlier = (destination[:, None] == destination[None, :]) & (
        position[None, :] < position[:, None]
    )
    rank_within = jnp.sum(earlier.astype(jnp.int32), axis=1)
    slot_index = destination * slots_each + rank_within
    slot_match = slot_index[:, None] == jnp.arange(total_slots, dtype=jnp.int32)[None, :]
    slot_table = slot_match.astype(jnp.float32)
    tile_plus = target_tile.reshape(pair_count) + 1
    sent_tiles = jnp.sum(jnp.where(slot_match, tile_plus[:, None], 0), axis=0) - 1
    owned_tiles = lax.all_to_all(
        sent_tiles.reshape(devices, slots_each),
        ("sec", "blk"),
        split_axis=0,
        concat_axis=0,
        tiled=True,
    ).reshape(total_slots)
    owner_table = (
        owned_tiles[:, None] == jnp.arange(shell_tiles, dtype=jnp.int32)[None, :]
    ).astype(jnp.float32)
    live_mask = (jnp.arange(wall_tiles, dtype=jnp.int32) < live_tiles[0]).astype(jnp.float32)
    column_table = (
        stiff_columns[:, :, None] == jnp.arange(shell_tiles + 2, dtype=jnp.int32)[None, None, :]
    ).astype(jnp.float32)

    def send_forth(buffer):
        arrived = lax.all_to_all(buffer, ("sec", "blk"), split_axis=0, concat_axis=0, tiled=True)
        return arrived

    def shell_forces(wall_value):
        traction = wall_normal * wall_value[None]
        traction_tiles = traction.reshape(3, wall_tiles, tile_size)
        contribution = jnp.einsum(
            "rkqn,crq->rkcn", interpolation, traction_tiles, precision=HIGH
        )
        contribution = contribution * live_mask[:, None, None, None]
        outgoing = jnp.einsum(
            "pm,pcn->mcn",
            slot_table,
            contribution.reshape(pair_count, 3, tile_size),
            precision=HIGHEST,
        )
        arrived = send_forth(outgoing.reshape(devices, slots_each, 3, tile_size)).reshape(
            total_slots, 3, tile_size
        )
        forces = jnp.einsum("ms,mcn->csn", owner_table, arrived, precision=HIGHEST)
        return forces.reshape(3, shell_tiles * tile_size)

    def off_diagonal(values):
        window = with_halo(values, ((("sec", "blk"), 1),), tile_size)
        window_tiles = window.reshape(3, shell_tiles + 2, tile_size)
        chosen = jnp.take(window_tiles, stiff_columns, axis=1)
        result = jnp.einsum("ibmn,cibn->cim", stiff_tiles, chosen, precision=HIGH)
        return result.reshape(3, shell_tiles * tile_size)

    def shell_update(current, wall_value):
        forces = shell_forces(wall_value)
        estimate = current
        for sweep_index in range(SWEEPS):
            estimate = (forces - off_diagonal(estimate)) / stiff_diagonal
        return (1.0 - RELAXATION) * current + RELAXATION * estimate

    wall_bottom = diffusivity[:, :, 0]
    wall_above = diffusivity[:, :, 1]
    jacobians = jnp.stack([first_jacobian, second_jacobian])
    first_section = apply_flux(
        face_rim(fluid_state), diffusivity, fluid_state, jacobians, 1.0, 0.0, TIME_STEP
    )
    settled = apply_flux(
        face_rim(first_section), diffusivity, fluid_state, jacobians, 0.5, 0.5, 0.5 * TIME_STEP
    )
    settled = lax.optimization_barrier(settled)
    settled_wall = settled[4, :, :, 0]
    half_square = 0.5 * TIME_STEP * TIME_STEP
    edge_rows = jnp.array([1.0, 0.0, 0.0, 0.0, 1.0], jnp.float32)

    def wall_state(motion_plane):
        source = motion_plane * wall_bottom[None]
        (east_side, west_side), (north_side, south_side) = plane_sides(source)
        first_step = 0.5 * (east_side - west_side)
        second_step = 0.5 * (north_side - south_side)
        first_flux = flat_blend(first_jacobian[:, 1:4], first_step)
        second_flux = flat_blend(second_jacobian[:, 1:4], second_step)
        return source, east_side + west_side + north_side + south_side, first_flux, second_flux

    current = displacement
    for iteration in range(ITERS):
        shell_blocks = current.reshape(3, shell_tiles, tile_size)
        reply_tiles = jnp.einsum("ms,csn->mcn", owner_table, shell_blocks, precision=HIGHEST)
        returned = lax.all_to_all(
            reply_tiles.reshape(devices, slots_each, 3, tile_size),
            ("sec", "blk"),
            split_axis=0,
            concat_axis=0,
            tiled=True,
        )
        interface_returned = returned.reshape(total_slots, 3, tile_size)
        pair_values = jnp.einsum("pm,mcn->pcn", slot_table, interface_returned, precision=HIGHEST)
        pair_values = pair_values.reshape(wall_tiles, fan_tiles, 3, tile_size)
        motion = (
            jnp.einsum("rkqn,rkcn->rcq", interpolation, pair_values, precision=HIGH)
            * live_mask[:, None, None]
        )
        motion_plane = motion.transpose(1, 0, 2).reshape(3, rows_first, rows_second)
        source, neighbours, first_flux, second_flux = wall_state(motion_plane)
        wall_value = settled_wall - half_square * (first_flux[4] + second_flux[4])
        current = shell_update(current, wall_value)
    bottom = TIME_STEP * source + half_square * (
        wall_bottom[None] * (neighbours - 6.0 * source) - first_flux[1:4] - second_flux[1:4]
    )
    above = half_square * wall_above[None] * source
    zero_plane = jnp.zeros_like(source[:1])
    bottom = jnp.concatenate([zero_plane, bottom, zero_plane], axis=0)
    bottom = bottom - half_square * (first_flux + second_flux) * edge_rows[:, None, None]
    above = jnp.concatenate([zero_plane, above, zero_plane], axis=0)
    depth = lax.broadcasted_iota(jnp.int32, settled.shape, 3)
    fluid_field = settled + jnp.where(
        depth == 0, bottom[..., None], jnp.where(depth == 1, above[..., None], 0.0)
    )
    return (fluid_field, current)


def solution(mesh):
    return jax.shard_map(
        local,
        mesh=mesh,
        in_specs=(
            P(None, "sec", "blk", None),
            P("sec", "blk", None),
            P(),
            P(),
            P(None, "sec", "blk"),
            P(("sec", "blk"), None, None, None),
            P(("sec", "blk"), None),
            P(("sec", "blk"), None),
            P(("sec", "blk")),
            P(None, ("sec", "blk")),
            P(None, ("sec", "blk")),
            P(("sec", "blk"), None, None, None),
            P(("sec", "blk"), None),
        ),
        out_specs=(P(None, "sec", "blk", None), P(None, ("sec", "blk"))),
        check_vma=False,
    )
```

```python
import functools

import jax
import jax.numpy as jnp
from jax import lax
from jax.experimental import pallas as pl
from jax.experimental.pallas import tpu as pltpu
from jax.sharding import PartitionSpec as P

ITERS = 3
SWEEPS = 3


TIME_STEP = 0.04
RELAXATION = 0.5
HIGHEST = lax.Precision.HIGHEST
HIGH = lax.Precision.HIGH


def with_halo(array, sides, width):
    for axis, dim in sides:
        size, length = (lax.axis_size(axis), array.shape[dim])
        up = [(i, (i + 1) % size) for i in range(size - 1)]
        down = [(j, i) for i, j in up]
        last = lax.slice_in_dim(array, length - width, length, axis=dim)
        first = lax.slice_in_dim(array, 0, width, axis=dim)
        before = lax.ppermute(last, axis, up)
        after = lax.ppermute(first, axis, down)
        array = jnp.concatenate([before, array, after], axis=dim)
    return array


def homogeneous(padded, diffusivity, first_jacobian, second_jacobian):
    centre = padded[:, 1:-1, 1:-1]
    east_side = padded[:, 2:, 1:-1]
    west_side = padded[:, :-2, 1:-1]
    north_side = padded[:, 1:-1, 2:]
    south_side = padded[:, 1:-1, :-2]
    zero_layer = jnp.zeros(centre.shape[:-1] + (1,), jnp.float32)
    upper_side = jnp.concatenate([centre[..., 1:], zero_layer], axis=3)
    lower_side = jnp.concatenate([zero_layer, centre[..., :-1]], axis=3)
    laplace = (
        east_side + west_side + north_side + south_side + upper_side + lower_side - 6.0 * centre
    )
    first_flux = jnp.einsum(
        "cd,dxyz->cxyz", first_jacobian, 0.5 * (east_side - west_side), precision=HIGH
    )
    second_flux = jnp.einsum(
        "cd,dxyz->cxyz", second_jacobian, 0.5 * (north_side - south_side), precision=HIGH
    )
    return diffusivity[None] * laplace - first_flux - second_flux


def flat_blend(jacobian, values):
    total = jacobian[:, 0, None, None] * values[0][None]
    for d in range(1, values.shape[0]):
        total = total + jacobian[:, d, None, None] * values[d][None]
    return total


def mixed(jacobian, row, values):
    total = jacobian[row, 0] * values[0]
    for d in range(1, values.shape[0]):
        total = total + jacobian[row, d] * values[d]
    return total


def flux_kernel(
    jac_ref, field_ref, west_ref, east_ref, south_ref, north_ref, dif_ref, extra_ref, out_ref,
    *, keep, blend, rate
):
    comps, rows, cols, depth = out_ref.shape
    lanes = lax.broadcasted_iota(jnp.int32, (cols, depth), 1)
    sublanes = lax.broadcasted_iota(jnp.int32, (cols, depth), 0)
    top = lanes == depth - 1
    bottom = lanes == 0
    last_col = sublanes == cols - 1
    first_col = sublanes == 0

    def row(x, carry):
        dif = dif_ref[x]
        steps_x, steps_y, laps = [], [], []
        for d in range(comps):
            centre = field_ref[d, x]
            east = jnp.where(x == rows - 1, east_ref[d, 0], field_ref[d, jnp.minimum(x + 1, rows - 1)])
            west = jnp.where(x == 0, west_ref[d, 0], field_ref[d, jnp.maximum(x - 1, 0)])
            north = jnp.where(last_col, north_ref[d, x], pltpu.roll(centre, cols - 1, 0))
            south = jnp.where(first_col, south_ref[d, x], pltpu.roll(centre, 1, 0))
            upper = jnp.where(top, 0.0, pltpu.roll(centre, depth - 1, 1))
            lower = jnp.where(bottom, 0.0, pltpu.roll(centre, 1, 1))
            laps.append((east + west + north + south + upper + lower - 6.0 * centre, centre))
            steps_x.append(0.5 * (east - west))
            steps_y.append(0.5 * (north - south))
        for c in range(comps):
            flux = jac_ref[0, c, 0] * steps_x[0]
            for d in range(1, comps):
                flux = flux + jac_ref[0, c, d] * steps_x[d]
            for d in range(comps):
                flux = flux + jac_ref[1, c, d] * steps_y[d]
            lap, centre = laps[c]
            value = keep * centre + rate * (dif * lap - flux)
            if blend:
                value = value + blend * extra_ref[c, x]
            out_ref[c, x] = value
        return carry

    lax.fori_loop(0, rows, row, 0, unroll=2)


def face_pieces(field):
    pieces = []
    for axis, dim in (("sec", 1), ("blk", 2)):
        size, length = (lax.axis_size(axis), field.shape[dim])
        up = [(i, i + 1) for i in range(size - 1)]
        down = [(j, i) for i, j in up]
        pieces.append(lax.ppermute(lax.slice_in_dim(field, length - 1, length, axis=dim), axis, up))
        pieces.append(lax.ppermute(lax.slice_in_dim(field, 0, 1, axis=dim), axis, down))
    return pieces


def apply_flux(field, diffusivity, extra, jacobians, keep, blend, rate, interpret=False, pieces=None):
    if pieces is None:
        pieces = face_pieces(field)
    out_shape = jax.ShapeDtypeStruct(field.shape, jnp.float32)
    vmem = pl.BlockSpec(memory_space=pltpu.VMEM)
    return pl.pallas_call(
        functools.partial(flux_kernel, keep=keep, blend=blend, rate=rate),
        out_shape=out_shape,
        in_specs=[pl.BlockSpec(memory_space=pltpu.SMEM)] + [vmem] * 7,
        out_specs=vmem,
        interpret=interpret,
    )(jacobians, field, *pieces, diffusivity, extra)

def face_rim(field):
    pieces = {}
    for axis, dim in (("sec", 1), ("blk", 2)):
        size, length = (lax.axis_size(axis), field.shape[dim])
        up = [(i, i + 1) for i in range(size - 1)]
        down = [(j, i) for i, j in up]
        before = lax.ppermute(lax.slice_in_dim(field, length - 1, length, axis=dim), axis, up)
        after = lax.ppermute(lax.slice_in_dim(field, 0, 1, axis=dim), axis, down)
        pieces[dim] = (before, after)
    middle = jnp.concatenate([pieces[2][0], field, pieces[2][1]], axis=2)
    corner = jnp.zeros(field.shape[:1] + (1, 1) + field.shape[3:], field.dtype)
    before_x, after_x = (jnp.concatenate([corner, edge, corner], axis=2) for edge in pieces[1])
    return jnp.concatenate([before_x, middle, after_x], axis=1)


def plane_sides(plane):
    sides = []
    for axis, dim in (("sec", 1), ("blk", 2)):
        size, length = (lax.axis_size(axis), plane.shape[dim])
        up = [(i, i + 1) for i in range(size - 1)]
        down = [(j, i) for i, j in up]
        before = lax.ppermute(lax.slice_in_dim(plane, length - 1, length, axis=dim), axis, up)
        after = lax.ppermute(lax.slice_in_dim(plane, 0, 1, axis=dim), axis, down)
        ahead = jnp.concatenate([lax.slice_in_dim(plane, 1, length, axis=dim), after], axis=dim)
        behind = jnp.concatenate([before, lax.slice_in_dim(plane, 0, length - 1, axis=dim)], axis=dim)
        sides.append((ahead, behind))
    return sides


def local(
    fluid_state,
    diffusivity,
    first_jacobian,
    second_jacobian,
    wall_normal,
    interpolation,
    target_device,
    target_tile,
    live_tiles,
    displacement,
    stiff_diagonal,
    stiff_tiles,
    stiff_columns,
):
    devices = lax.axis_size(("sec", "blk"))
    wall_tiles = interpolation.shape[0]
    fan_tiles = interpolation.shape[1]
    tile_size = interpolation.shape[2]
    slots_each = 2 * wall_tiles * fan_tiles // devices
    total_slots = devices * slots_each
    pair_count = wall_tiles * fan_tiles
    shell_tiles = displacement.shape[1] // tile_size
    rows_first = fluid_state.shape[1]
    rows_second = fluid_state.shape[2]
    destination = target_device.reshape(pair_count)
    position = jnp.arange(pair_count, dtype=jnp.int32)
    earlier = (destination[:, None] == destination[None, :]) & (
        position[None, :] < position[:, None]
    )
    rank_within = jnp.sum(earlier.astype(jnp.int32), axis=1)
    slot_index = destination * slots_each + rank_within
    slot_match = slot_index[:, None] == jnp.arange(total_slots, dtype=jnp.int32)[None, :]
    slot_table = slot_match.astype(jnp.float32)
    tile_plus = target_tile.reshape(pair_count) + 1
    sent_tiles = jnp.sum(jnp.where(slot_match, tile_plus[:, None], 0), axis=0) - 1
    owned_tiles = lax.all_to_all(
        sent_tiles.reshape(devices, slots_each),
        ("sec", "blk"),
        split_axis=0,
        concat_axis=0,
        tiled=True,
    ).reshape(total_slots)
    owner_table = (
        owned_tiles[:, None] == jnp.arange(shell_tiles, dtype=jnp.int32)[None, :]
    ).astype(jnp.float32)
    live_mask = (jnp.arange(wall_tiles, dtype=jnp.int32) < live_tiles[0]).astype(jnp.float32)
    column_table = (
        stiff_columns[:, :, None] == jnp.arange(shell_tiles + 2, dtype=jnp.int32)[None, None, :]
    ).astype(jnp.float32)

    def send_forth(buffer):
        arrived = lax.all_to_all(buffer, ("sec", "blk"), split_axis=0, concat_axis=0, tiled=True)
        return arrived

    def shell_forces(wall_value):
        traction = wall_normal * wall_value[None]
        traction_tiles = traction.reshape(3, wall_tiles, tile_size)
        contribution = jnp.einsum(
            "rkqn,crq->rkcn", interpolation, traction_tiles, precision=HIGH
        )
        contribution = contribution * live_mask[:, None, None, None]
        outgoing = jnp.einsum(
            "pm,pcn->mcn",
            slot_table,
            contribution.reshape(pair_count, 3, tile_size),
            precision=HIGHEST,
        )
        arrived = send_forth(outgoing.reshape(devices, slots_each, 3, tile_size)).reshape(
            total_slots, 3, tile_size
        )
        forces = jnp.einsum("ms,mcn->csn", owner_table, arrived, precision=HIGHEST)
        return forces.reshape(3, shell_tiles * tile_size)

    def off_diagonal(values):
        window = with_halo(values, ((("sec", "blk"), 1),), tile_size)
        window_tiles = window.reshape(3, shell_tiles + 2, tile_size)
        chosen = jnp.einsum("ibj,cjn->ibcn", column_table, window_tiles, precision=HIGHEST)
        result = jnp.einsum("ibmn,ibcn->cim", stiff_tiles, chosen, precision=HIGH)
        return result.reshape(3, shell_tiles * tile_size)

    def shell_update(current, wall_value):
        forces = shell_forces(wall_value)
        estimate = current
        for sweep_index in range(SWEEPS):
            estimate = (forces - off_diagonal(estimate)) / stiff_diagonal
        return (1.0 - RELAXATION) * current + RELAXATION * estimate

    wall_bottom = diffusivity[:, :, 0]
    wall_above = diffusivity[:, :, 1]
    jacobians = jnp.stack([first_jacobian, second_jacobian])
    first_section = apply_flux(
        fluid_state, diffusivity, fluid_state, jacobians, 1.0, 0.0, TIME_STEP
    )
    settled = apply_flux(
        first_section, diffusivity, fluid_state, jacobians, 0.5, 0.5, 0.5 * TIME_STEP
    )
    settled = lax.optimization_barrier(settled)
    settled_wall = settled[4, :, :, 0]
    half_square = 0.5 * TIME_STEP * TIME_STEP
    edge_rows = jnp.array([1.0, 0.0, 0.0, 0.0, 1.0], jnp.float32)

    def wall_state(motion_plane):
        source = motion_plane * wall_bottom[None]
        (east_side, west_side), (north_side, south_side) = plane_sides(source)
        first_step = 0.5 * (east_side - west_side)
        second_step = 0.5 * (north_side - south_side)
        first_flux = flat_blend(first_jacobian[:, 1:4], first_step)
        second_flux = flat_blend(second_jacobian[:, 1:4], second_step)
        return source, east_side + west_side + north_side + south_side, first_flux, second_flux

    current = displacement
    for iteration in range(ITERS):
        shell_blocks = current.reshape(3, shell_tiles, tile_size)
        reply_tiles = jnp.einsum("ms,csn->mcn", owner_table, shell_blocks, precision=HIGHEST)
        returned = lax.all_to_all(
            reply_tiles.reshape(devices, slots_each, 3, tile_size),
            ("sec", "blk"),
            split_axis=0,
            concat_axis=0,
            tiled=True,
        )
        interface_returned = returned.reshape(total_slots, 3, tile_size)
        pair_values = jnp.einsum("pm,mcn->pcn", slot_table, interface_returned, precision=HIGHEST)
        pair_values = pair_values.reshape(wall_tiles, fan_tiles, 3, tile_size)
        motion = (
            jnp.einsum("rkqn,rkcn->rcq", interpolation, pair_values, precision=HIGH)
            * live_mask[:, None, None]
        )
        motion_plane = motion.transpose(1, 0, 2).reshape(3, rows_first, rows_second)
        source, neighbours, first_flux, second_flux = wall_state(motion_plane)
        wall_value = settled_wall - half_square * (first_flux[4] + second_flux[4])
        current = shell_update(current, wall_value)
    bottom = TIME_STEP * source + half_square * (
        wall_bottom[None] * (neighbours - 6.0 * source) - first_flux[1:4] - second_flux[1:4]
    )
    above = half_square * wall_above[None] * source
    zero_plane = jnp.zeros_like(source[:1])
    bottom = jnp.concatenate([zero_plane, bottom, zero_plane], axis=0)
    bottom = bottom - half_square * (first_flux + second_flux) * edge_rows[:, None, None]
    above = jnp.concatenate([zero_plane, above, zero_plane], axis=0)
    depth = lax.broadcasted_iota(jnp.int32, settled.shape, 3)
    fluid_field = settled + jnp.where(
        depth == 0, bottom[..., None], jnp.where(depth == 1, above[..., None], 0.0)
    )
    return (fluid_field, current)


def solution(mesh):
    return jax.shard_map(
        local,
        mesh=mesh,
        in_specs=(
            P(None, "sec", "blk", None),
            P("sec", "blk", None),
            P(),
            P(),
            P(None, "sec", "blk"),
            P(("sec", "blk"), None, None, None),
            P(("sec", "blk"), None),
            P(("sec", "blk"), None),
            P(("sec", "blk")),
            P(None, ("sec", "blk")),
            P(None, ("sec", "blk")),
            P(("sec", "blk"), None, None, None),
            P(("sec", "blk"), None),
        ),
        out_specs=(P(None, "sec", "blk", None), P(None, ("sec", "blk"))),
        check_vma=False,
    )
```

```python
import functools

import jax
import jax.numpy as jnp
from jax import lax
from jax.experimental import pallas as pl
from jax.experimental.pallas import tpu as pltpu
from jax.sharding import PartitionSpec as P

ITERS = 3
SWEEPS = 3


TIME_STEP = 0.04
RELAXATION = 0.5
HIGHEST = lax.Precision.HIGHEST
HIGH = lax.Precision.HIGH


def with_halo(array, sides, width):
    for axis, dim in sides:
        size, length = (lax.axis_size(axis), array.shape[dim])
        up = [(i, (i + 1) % size) for i in range(size - 1)]
        down = [(j, i) for i, j in up]
        last = lax.slice_in_dim(array, length - width, length, axis=dim)
        first = lax.slice_in_dim(array, 0, width, axis=dim)
        before = lax.ppermute(last, axis, up)
        after = lax.ppermute(first, axis, down)
        array = jnp.concatenate([before, array, after], axis=dim)
    return array


def homogeneous(padded, diffusivity, first_jacobian, second_jacobian):
    centre = padded[:, 1:-1, 1:-1]
    east_side = padded[:, 2:, 1:-1]
    west_side = padded[:, :-2, 1:-1]
    north_side = padded[:, 1:-1, 2:]
    south_side = padded[:, 1:-1, :-2]
    zero_layer = jnp.zeros(centre.shape[:-1] + (1,), jnp.float32)
    upper_side = jnp.concatenate([centre[..., 1:], zero_layer], axis=3)
    lower_side = jnp.concatenate([zero_layer, centre[..., :-1]], axis=3)
    laplace = (
        east_side + west_side + north_side + south_side + upper_side + lower_side - 6.0 * centre
    )
    first_flux = jnp.einsum(
        "cd,dxyz->cxyz", first_jacobian, 0.5 * (east_side - west_side), precision=HIGH
    )
    second_flux = jnp.einsum(
        "cd,dxyz->cxyz", second_jacobian, 0.5 * (north_side - south_side), precision=HIGH
    )
    return diffusivity[None] * laplace - first_flux - second_flux


def flat_blend(jacobian, values):
    total = jacobian[:, 0, None, None] * values[0][None]
    for d in range(1, values.shape[0]):
        total = total + jacobian[:, d, None, None] * values[d][None]
    return total


def mixed(jacobian, row, values):
    total = jacobian[row, 0] * values[0]
    for d in range(1, values.shape[0]):
        total = total + jacobian[row, d] * values[d]
    return total


def flux_kernel(
    jac_ref, field_ref, west_ref, east_ref, south_ref, north_ref, dif_ref, extra_ref, out_ref,
    *, keep, blend, rate
):
    comps, rows, cols, depth = out_ref.shape
    lanes = lax.broadcasted_iota(jnp.int32, (cols, depth), 1)
    sublanes = lax.broadcasted_iota(jnp.int32, (cols, depth), 0)
    top = lanes == depth - 1
    bottom = lanes == 0
    last_col = sublanes == cols - 1
    first_col = sublanes == 0

    def row(x, carry):
        dif = dif_ref[x]
        steps_x, steps_y, laps = [], [], []
        for d in range(comps):
            centre = field_ref[d, x]
            east = jnp.where(x == rows - 1, east_ref[d, 0], field_ref[d, jnp.minimum(x + 1, rows - 1)])
            west = jnp.where(x == 0, west_ref[d, 0], field_ref[d, jnp.maximum(x - 1, 0)])
            north = jnp.where(last_col, north_ref[d, x], pltpu.roll(centre, cols - 1, 0))
            south = jnp.where(first_col, south_ref[d, x], pltpu.roll(centre, 1, 0))
            upper = jnp.where(top, 0.0, pltpu.roll(centre, depth - 1, 1))
            lower = jnp.where(bottom, 0.0, pltpu.roll(centre, 1, 1))
            laps.append((east + west + north + south + upper + lower - 6.0 * centre, centre))
            steps_x.append(0.5 * (east - west))
            steps_y.append(0.5 * (north - south))
        for c in range(comps):
            flux = jac_ref[0, c, 0] * steps_x[0]
            for d in range(1, comps):
                flux = flux + jac_ref[0, c, d] * steps_x[d]
            for d in range(comps):
                flux = flux + jac_ref[1, c, d] * steps_y[d]
            lap, centre = laps[c]
            value = keep * centre + rate * (dif * lap - flux)
            if blend:
                value = value + blend * extra_ref[c, x]
            out_ref[c, x] = value
        return carry

    lax.fori_loop(0, rows, row, 0, unroll=4)


def face_pieces(field):
    pieces = []
    for axis, dim in (("sec", 1), ("blk", 2)):
        size, length = (lax.axis_size(axis), field.shape[dim])
        up = [(i, i + 1) for i in range(size - 1)]
        down = [(j, i) for i, j in up]
        pieces.append(lax.ppermute(lax.slice_in_dim(field, length - 1, length, axis=dim), axis, up))
        pieces.append(lax.ppermute(lax.slice_in_dim(field, 0, 1, axis=dim), axis, down))
    return pieces


def apply_flux(field, diffusivity, extra, jacobians, keep, blend, rate, interpret=False, pieces=None):
    if pieces is None:
        pieces = face_pieces(field)
    out_shape = jax.ShapeDtypeStruct(field.shape, jnp.float32)
    vmem = pl.BlockSpec(memory_space=pltpu.VMEM)
    return pl.pallas_call(
        functools.partial(flux_kernel, keep=keep, blend=blend, rate=rate),
        out_shape=out_shape,
        in_specs=[pl.BlockSpec(memory_space=pltpu.SMEM)] + [vmem] * 7,
        out_specs=vmem,
        interpret=interpret,
    )(jacobians, field, *pieces, diffusivity, extra)

def face_rim(field):
    pieces = {}
    for axis, dim in (("sec", 1), ("blk", 2)):
        size, length = (lax.axis_size(axis), field.shape[dim])
        up = [(i, i + 1) for i in range(size - 1)]
        down = [(j, i) for i, j in up]
        before = lax.ppermute(lax.slice_in_dim(field, length - 1, length, axis=dim), axis, up)
        after = lax.ppermute(lax.slice_in_dim(field, 0, 1, axis=dim), axis, down)
        pieces[dim] = (before, after)
    middle = jnp.concatenate([pieces[2][0], field, pieces[2][1]], axis=2)
    corner = jnp.zeros(field.shape[:1] + (1, 1) + field.shape[3:], field.dtype)
    before_x, after_x = (jnp.concatenate([corner, edge, corner], axis=2) for edge in pieces[1])
    return jnp.concatenate([before_x, middle, after_x], axis=1)


def plane_sides(plane):
    sides = []
    for axis, dim in (("sec", 1), ("blk", 2)):
        size, length = (lax.axis_size(axis), plane.shape[dim])
        up = [(i, i + 1) for i in range(size - 1)]
        down = [(j, i) for i, j in up]
        before = lax.ppermute(lax.slice_in_dim(plane, length - 1, length, axis=dim), axis, up)
        after = lax.ppermute(lax.slice_in_dim(plane, 0, 1, axis=dim), axis, down)
        ahead = jnp.concatenate([lax.slice_in_dim(plane, 1, length, axis=dim), after], axis=dim)
        behind = jnp.concatenate([before, lax.slice_in_dim(plane, 0, length - 1, axis=dim)], axis=dim)
        sides.append((ahead, behind))
    return sides


def local(
    fluid_state,
    diffusivity,
    first_jacobian,
    second_jacobian,
    wall_normal,
    interpolation,
    target_device,
    target_tile,
    live_tiles,
    displacement,
    stiff_diagonal,
    stiff_tiles,
    stiff_columns,
):
    devices = lax.axis_size(("sec", "blk"))
    wall_tiles = interpolation.shape[0]
    fan_tiles = interpolation.shape[1]
    tile_size = interpolation.shape[2]
    slots_each = 2 * wall_tiles * fan_tiles // devices
    total_slots = devices * slots_each
    pair_count = wall_tiles * fan_tiles
    shell_tiles = displacement.shape[1] // tile_size
    rows_first = fluid_state.shape[1]
    rows_second = fluid_state.shape[2]
    destination = target_device.reshape(pair_count)
    position = jnp.arange(pair_count, dtype=jnp.int32)
    earlier = (destination[:, None] == destination[None, :]) & (
        position[None, :] < position[:, None]
    )
    rank_within = jnp.sum(earlier.astype(jnp.int32), axis=1)
    slot_index = destination * slots_each + rank_within
    slot_match = slot_index[:, None] == jnp.arange(total_slots, dtype=jnp.int32)[None, :]
    slot_table = slot_match.astype(jnp.float32)
    tile_plus = target_tile.reshape(pair_count) + 1
    sent_tiles = jnp.sum(jnp.where(slot_match, tile_plus[:, None], 0), axis=0) - 1
    owned_tiles = lax.all_to_all(
        sent_tiles.reshape(devices, slots_each),
        ("sec", "blk"),
        split_axis=0,
        concat_axis=0,
        tiled=True,
    ).reshape(total_slots)
    owner_table = (
        owned_tiles[:, None] == jnp.arange(shell_tiles, dtype=jnp.int32)[None, :]
    ).astype(jnp.float32)
    live_mask = (jnp.arange(wall_tiles, dtype=jnp.int32) < live_tiles[0]).astype(jnp.float32)
    column_table = (
        stiff_columns[:, :, None] == jnp.arange(shell_tiles + 2, dtype=jnp.int32)[None, None, :]
    ).astype(jnp.float32)

    def send_forth(buffer):
        arrived = lax.all_to_all(buffer, ("sec", "blk"), split_axis=0, concat_axis=0, tiled=True)
        return arrived

    def shell_forces(wall_value):
        traction = wall_normal * wall_value[None]
        traction_tiles = traction.reshape(3, wall_tiles, tile_size)
        contribution = jnp.einsum(
            "rkqn,crq->rkcn", interpolation, traction_tiles, precision=HIGH
        )
        contribution = contribution * live_mask[:, None, None, None]
        outgoing = jnp.einsum(
            "pm,pcn->mcn",
            slot_table,
            contribution.reshape(pair_count, 3, tile_size),
            precision=HIGHEST,
        )
        arrived = send_forth(outgoing.reshape(devices, slots_each, 3, tile_size)).reshape(
            total_slots, 3, tile_size
        )
        forces = jnp.einsum("ms,mcn->csn", owner_table, arrived, precision=HIGHEST)
        return forces.reshape(3, shell_tiles * tile_size)

    def off_diagonal(values):
        window = with_halo(values, ((("sec", "blk"), 1),), tile_size)
        window_tiles = window.reshape(3, shell_tiles + 2, tile_size)
        chosen = jnp.einsum("ibj,cjn->ibcn", column_table, window_tiles, precision=HIGHEST)
        result = jnp.einsum("ibmn,ibcn->cim", stiff_tiles, chosen, precision=HIGH)
        return result.reshape(3, shell_tiles * tile_size)

    def shell_update(current, wall_value):
        forces = shell_forces(wall_value)
        estimate = current
        for sweep_index in range(SWEEPS):
            estimate = (forces - off_diagonal(estimate)) / stiff_diagonal
        return (1.0 - RELAXATION) * current + RELAXATION * estimate

    wall_bottom = diffusivity[:, :, 0]
    wall_above = diffusivity[:, :, 1]
    jacobians = jnp.stack([first_jacobian, second_jacobian])
    first_section = apply_flux(
        fluid_state, diffusivity, fluid_state, jacobians, 1.0, 0.0, TIME_STEP
    )
    settled = apply_flux(
        first_section, diffusivity, fluid_state, jacobians, 0.5, 0.5, 0.5 * TIME_STEP
    )
    settled = lax.optimization_barrier(settled)
    settled_wall = settled[4, :, :, 0]
    half_square = 0.5 * TIME_STEP * TIME_STEP
    edge_rows = jnp.array([1.0, 0.0, 0.0, 0.0, 1.0], jnp.float32)

    def wall_state(motion_plane):
        source = motion_plane * wall_bottom[None]
        (east_side, west_side), (north_side, south_side) = plane_sides(source)
        first_step = 0.5 * (east_side - west_side)
        second_step = 0.5 * (north_side - south_side)
        first_flux = flat_blend(first_jacobian[:, 1:4], first_step)
        second_flux = flat_blend(second_jacobian[:, 1:4], second_step)
        return source, east_side + west_side + north_side + south_side, first_flux, second_flux

    current = displacement
    for iteration in range(ITERS):
        shell_blocks = current.reshape(3, shell_tiles, tile_size)
        reply_tiles = jnp.einsum("ms,csn->mcn", owner_table, shell_blocks, precision=HIGHEST)
        returned = lax.all_to_all(
            reply_tiles.reshape(devices, slots_each, 3, tile_size),
            ("sec", "blk"),
            split_axis=0,
            concat_axis=0,
            tiled=True,
        )
        interface_returned = returned.reshape(total_slots, 3, tile_size)
        pair_values = jnp.einsum("pm,mcn->pcn", slot_table, interface_returned, precision=HIGHEST)
        pair_values = pair_values.reshape(wall_tiles, fan_tiles, 3, tile_size)
        motion = (
            jnp.einsum("rkqn,rkcn->rcq", interpolation, pair_values, precision=HIGH)
            * live_mask[:, None, None]
        )
        motion_plane = motion.transpose(1, 0, 2).reshape(3, rows_first, rows_second)
        source, neighbours, first_flux, second_flux = wall_state(motion_plane)
        wall_value = settled_wall - half_square * (first_flux[4] + second_flux[4])
        current = shell_update(current, wall_value)
    bottom = TIME_STEP * source + half_square * (
        wall_bottom[None] * (neighbours - 6.0 * source) - first_flux[1:4] - second_flux[1:4]
    )
    above = half_square * wall_above[None] * source
    zero_plane = jnp.zeros_like(source[:1])
    bottom = jnp.concatenate([zero_plane, bottom, zero_plane], axis=0)
    bottom = bottom - half_square * (first_flux + second_flux) * edge_rows[:, None, None]
    above = jnp.concatenate([zero_plane, above, zero_plane], axis=0)
    depth = lax.broadcasted_iota(jnp.int32, settled.shape, 3)
    fluid_field = settled + jnp.where(
        depth == 0, bottom[..., None], jnp.where(depth == 1, above[..., None], 0.0)
    )
    return (fluid_field, current)


def solution(mesh):
    return jax.shard_map(
        local,
        mesh=mesh,
        in_specs=(
            P(None, "sec", "blk", None),
            P("sec", "blk", None),
            P(),
            P(),
            P(None, "sec", "blk"),
            P(("sec", "blk"), None, None, None),
            P(("sec", "blk"), None),
            P(("sec", "blk"), None),
            P(("sec", "blk")),
            P(None, ("sec", "blk")),
            P(None, ("sec", "blk")),
            P(("sec", "blk"), None, None, None),
            P(("sec", "blk"), None),
        ),
        out_specs=(P(None, "sec", "blk", None), P(None, ("sec", "blk"))),
        check_vma=False,
    )
```

```python
import functools

import jax
import jax.numpy as jnp
from jax import lax
from jax.experimental import pallas as pl
from jax.experimental.pallas import tpu as pltpu
from jax.sharding import PartitionSpec as P

ITERS = 3
SWEEPS = 3


TIME_STEP = 0.04
RELAXATION = 0.5
HIGHEST = lax.Precision.HIGHEST
HIGH = lax.Precision.HIGH


def with_halo(array, sides, width):
    for axis, dim in sides:
        size, length = (lax.axis_size(axis), array.shape[dim])
        up = [(i, (i + 1) % size) for i in range(size - 1)]
        down = [(j, i) for i, j in up]
        last = lax.slice_in_dim(array, length - width, length, axis=dim)
        first = lax.slice_in_dim(array, 0, width, axis=dim)
        before = lax.ppermute(last, axis, up)
        after = lax.ppermute(first, axis, down)
        array = jnp.concatenate([before, array, after], axis=dim)
    return array


def homogeneous(padded, diffusivity, first_jacobian, second_jacobian):
    centre = padded[:, 1:-1, 1:-1]
    east_side = padded[:, 2:, 1:-1]
    west_side = padded[:, :-2, 1:-1]
    north_side = padded[:, 1:-1, 2:]
    south_side = padded[:, 1:-1, :-2]
    zero_layer = jnp.zeros(centre.shape[:-1] + (1,), jnp.float32)
    upper_side = jnp.concatenate([centre[..., 1:], zero_layer], axis=3)
    lower_side = jnp.concatenate([zero_layer, centre[..., :-1]], axis=3)
    laplace = (
        east_side + west_side + north_side + south_side + upper_side + lower_side - 6.0 * centre
    )
    first_flux = jnp.einsum(
        "cd,dxyz->cxyz", first_jacobian, 0.5 * (east_side - west_side), precision=HIGH
    )
    second_flux = jnp.einsum(
        "cd,dxyz->cxyz", second_jacobian, 0.5 * (north_side - south_side), precision=HIGH
    )
    return diffusivity[None] * laplace - first_flux - second_flux


def flat_blend(jacobian, values):
    total = jacobian[:, 0, None, None] * values[0][None]
    for d in range(1, values.shape[0]):
        total = total + jacobian[:, d, None, None] * values[d][None]
    return total


def mixed(jacobian, row, values):
    total = jacobian[row, 0] * values[0]
    for d in range(1, values.shape[0]):
        total = total + jacobian[row, d] * values[d]
    return total


def flux_kernel(jac_ref, field_ref, west_ref, east_ref, south_ref, north_ref, dif_ref, *rest, keep, blend, rate):
    extra_ref, out_ref = rest if blend else (None, rest[0])
    comps, rows, cols, depth = out_ref.shape
    lanes = lax.broadcasted_iota(jnp.int32, (cols, depth), 1)
    sublanes = lax.broadcasted_iota(jnp.int32, (cols, depth), 0)
    top = lanes == depth - 1
    bottom = lanes == 0
    last_col = sublanes == cols - 1
    first_col = sublanes == 0

    def row(x, carry):
        dif = dif_ref[x]
        steps_x, steps_y, laps = [], [], []
        for d in range(comps):
            centre = field_ref[d, x]
            east = jnp.where(x == rows - 1, east_ref[d, 0], field_ref[d, jnp.minimum(x + 1, rows - 1)])
            west = jnp.where(x == 0, west_ref[d, 0], field_ref[d, jnp.maximum(x - 1, 0)])
            north = jnp.where(last_col, north_ref[d, x], pltpu.roll(centre, cols - 1, 0))
            south = jnp.where(first_col, south_ref[d, x], pltpu.roll(centre, 1, 0))
            upper = jnp.where(top, 0.0, pltpu.roll(centre, depth - 1, 1))
            lower = jnp.where(bottom, 0.0, pltpu.roll(centre, 1, 1))
            laps.append((east + west + north + south + upper + lower - 6.0 * centre, centre))
            steps_x.append(0.5 * (east - west))
            steps_y.append(0.5 * (north - south))
        for c in range(comps):
            flux = jac_ref[0, c, 0] * steps_x[0]
            for d in range(1, comps):
                flux = flux + jac_ref[0, c, d] * steps_x[d]
            for d in range(comps):
                flux = flux + jac_ref[1, c, d] * steps_y[d]
            lap, centre = laps[c]
            value = keep * centre + rate * (dif * lap - flux)
            if blend:
                value = value + blend * extra_ref[c, x]
            out_ref[c, x] = value
        return carry

    lax.fori_loop(0, rows, row, 0, unroll=2)


def face_pieces(field):
    pieces = []
    for axis, dim in (("sec", 1), ("blk", 2)):
        size, length = (lax.axis_size(axis), field.shape[dim])
        up = [(i, i + 1) for i in range(size - 1)]
        down = [(j, i) for i, j in up]
        pieces.append(lax.ppermute(lax.slice_in_dim(field, length - 1, length, axis=dim), axis, up))
        pieces.append(lax.ppermute(lax.slice_in_dim(field, 0, 1, axis=dim), axis, down))
    return pieces


def apply_flux(field, diffusivity, extra, jacobians, keep, blend, rate, interpret=False, pieces=None):
    if pieces is None:
        pieces = face_pieces(field)
    out_shape = jax.ShapeDtypeStruct(field.shape, jnp.float32)
    vmem = pl.BlockSpec(memory_space=pltpu.VMEM)
    return pl.pallas_call(
        functools.partial(flux_kernel, keep=keep, blend=blend, rate=rate),
        out_shape=out_shape,
        in_specs=[pl.BlockSpec(memory_space=pltpu.SMEM)] + [vmem] * (7 if blend else 6),
        out_specs=vmem,
        interpret=interpret,
    )(jacobians, field, *pieces, diffusivity, *([extra] if blend else []))

def face_rim(field):
    pieces = {}
    for axis, dim in (("sec", 1), ("blk", 2)):
        size, length = (lax.axis_size(axis), field.shape[dim])
        up = [(i, i + 1) for i in range(size - 1)]
        down = [(j, i) for i, j in up]
        before = lax.ppermute(lax.slice_in_dim(field, length - 1, length, axis=dim), axis, up)
        after = lax.ppermute(lax.slice_in_dim(field, 0, 1, axis=dim), axis, down)
        pieces[dim] = (before, after)
    middle = jnp.concatenate([pieces[2][0], field, pieces[2][1]], axis=2)
    corner = jnp.zeros(field.shape[:1] + (1, 1) + field.shape[3:], field.dtype)
    before_x, after_x = (jnp.concatenate([corner, edge, corner], axis=2) for edge in pieces[1])
    return jnp.concatenate([before_x, middle, after_x], axis=1)


def plane_sides(plane):
    sides = []
    for axis, dim in (("sec", 1), ("blk", 2)):
        size, length = (lax.axis_size(axis), plane.shape[dim])
        up = [(i, i + 1) for i in range(size - 1)]
        down = [(j, i) for i, j in up]
        before = lax.ppermute(lax.slice_in_dim(plane, length - 1, length, axis=dim), axis, up)
        after = lax.ppermute(lax.slice_in_dim(plane, 0, 1, axis=dim), axis, down)
        ahead = jnp.concatenate([lax.slice_in_dim(plane, 1, length, axis=dim), after], axis=dim)
        behind = jnp.concatenate([before, lax.slice_in_dim(plane, 0, length - 1, axis=dim)], axis=dim)
        sides.append((ahead, behind))
    return sides


def local(
    fluid_state,
    diffusivity,
    first_jacobian,
    second_jacobian,
    wall_normal,
    interpolation,
    target_device,
    target_tile,
    live_tiles,
    displacement,
    stiff_diagonal,
    stiff_tiles,
    stiff_columns,
):
    devices = lax.axis_size(("sec", "blk"))
    wall_tiles = interpolation.shape[0]
    fan_tiles = interpolation.shape[1]
    tile_size = interpolation.shape[2]
    slots_each = 2 * wall_tiles * fan_tiles // devices
    total_slots = devices * slots_each
    pair_count = wall_tiles * fan_tiles
    shell_tiles = displacement.shape[1] // tile_size
    rows_first = fluid_state.shape[1]
    rows_second = fluid_state.shape[2]
    destination = target_device.reshape(pair_count)
    position = jnp.arange(pair_count, dtype=jnp.int32)
    earlier = (destination[:, None] == destination[None, :]) & (
        position[None, :] < position[:, None]
    )
    rank_within = jnp.sum(earlier.astype(jnp.int32), axis=1)
    slot_index = destination * slots_each + rank_within
    slot_match = slot_index[:, None] == jnp.arange(total_slots, dtype=jnp.int32)[None, :]
    slot_table = slot_match.astype(jnp.float32)
    tile_plus = target_tile.reshape(pair_count) + 1
    sent_tiles = jnp.sum(jnp.where(slot_match, tile_plus[:, None], 0), axis=0) - 1
    owned_tiles = lax.all_to_all(
        sent_tiles.reshape(devices, slots_each),
        ("sec", "blk"),
        split_axis=0,
        concat_axis=0,
        tiled=True,
    ).reshape(total_slots)
    owner_table = (
        owned_tiles[:, None] == jnp.arange(shell_tiles, dtype=jnp.int32)[None, :]
    ).astype(jnp.float32)
    live_mask = (jnp.arange(wall_tiles, dtype=jnp.int32) < live_tiles[0]).astype(jnp.float32)
    column_table = (
        stiff_columns[:, :, None] == jnp.arange(shell_tiles + 2, dtype=jnp.int32)[None, None, :]
    ).astype(jnp.float32)

    def send_forth(buffer):
        arrived = lax.all_to_all(buffer, ("sec", "blk"), split_axis=0, concat_axis=0, tiled=True)
        return arrived

    def shell_forces(wall_value):
        traction = wall_normal * wall_value[None]
        traction_tiles = traction.reshape(3, wall_tiles, tile_size)
        contribution = jnp.einsum(
            "rkqn,crq->rkcn", interpolation, traction_tiles, precision=HIGH
        )
        contribution = contribution * live_mask[:, None, None, None]
        outgoing = jnp.einsum(
            "pm,pcn->mcn",
            slot_table,
            contribution.reshape(pair_count, 3, tile_size),
            precision=HIGHEST,
        )
        arrived = send_forth(outgoing.reshape(devices, slots_each, 3, tile_size)).reshape(
            total_slots, 3, tile_size
        )
        forces = jnp.einsum("ms,mcn->csn", owner_table, arrived, precision=HIGHEST)
        return forces.reshape(3, shell_tiles * tile_size)

    def off_diagonal(values):
        window = with_halo(values, ((("sec", "blk"), 1),), tile_size)
        window_tiles = window.reshape(3, shell_tiles + 2, tile_size)
        chosen = jnp.einsum("ibj,cjn->ibcn", column_table, window_tiles, precision=HIGHEST)
        result = jnp.einsum("ibmn,ibcn->cim", stiff_tiles, chosen, precision=HIGH)
        return result.reshape(3, shell_tiles * tile_size)

    def shell_update(current, wall_value):
        forces = shell_forces(wall_value)
        estimate = current
        for sweep_index in range(SWEEPS):
            estimate = (forces - off_diagonal(estimate)) / stiff_diagonal
        return (1.0 - RELAXATION) * current + RELAXATION * estimate

    wall_bottom = diffusivity[:, :, 0]
    wall_above = diffusivity[:, :, 1]
    jacobians = jnp.stack([first_jacobian, second_jacobian])
    first_section = apply_flux(
        fluid_state, diffusivity, fluid_state, jacobians, 1.0, 0.0, TIME_STEP
    )
    settled = apply_flux(
        first_section, diffusivity, fluid_state, jacobians, 0.5, 0.5, 0.5 * TIME_STEP
    )
    settled = lax.optimization_barrier(settled)
    settled_wall = settled[4, :, :, 0]
    half_square = 0.5 * TIME_STEP * TIME_STEP
    edge_rows = jnp.array([1.0, 0.0, 0.0, 0.0, 1.0], jnp.float32)

    def wall_state(motion_plane):
        source = motion_plane * wall_bottom[None]
        (east_side, west_side), (north_side, south_side) = plane_sides(source)
        first_step = 0.5 * (east_side - west_side)
        second_step = 0.5 * (north_side - south_side)
        first_flux = flat_blend(first_jacobian[:, 1:4], first_step)
        second_flux = flat_blend(second_jacobian[:, 1:4], second_step)
        return source, east_side + west_side + north_side + south_side, first_flux, second_flux

    current = displacement
    for iteration in range(ITERS):
        shell_blocks = current.reshape(3, shell_tiles, tile_size)
        reply_tiles = jnp.einsum("ms,csn->mcn", owner_table, shell_blocks, precision=HIGHEST)
        returned = lax.all_to_all(
            reply_tiles.reshape(devices, slots_each, 3, tile_size),
            ("sec", "blk"),
            split_axis=0,
            concat_axis=0,
            tiled=True,
        )
        interface_returned = returned.reshape(total_slots, 3, tile_size)
        pair_values = jnp.einsum("pm,mcn->pcn", slot_table, interface_returned, precision=HIGHEST)
        pair_values = pair_values.reshape(wall_tiles, fan_tiles, 3, tile_size)
        motion = (
            jnp.einsum("rkqn,rkcn->rcq", interpolation, pair_values, precision=HIGH)
            * live_mask[:, None, None]
        )
        motion_plane = motion.transpose(1, 0, 2).reshape(3, rows_first, rows_second)
        source, neighbours, first_flux, second_flux = wall_state(motion_plane)
        wall_value = settled_wall - half_square * (first_flux[4] + second_flux[4])
        current = shell_update(current, wall_value)
    bottom = TIME_STEP * source + half_square * (
        wall_bottom[None] * (neighbours - 6.0 * source) - first_flux[1:4] - second_flux[1:4]
    )
    above = half_square * wall_above[None] * source
    zero_plane = jnp.zeros_like(source[:1])
    bottom = jnp.concatenate([zero_plane, bottom, zero_plane], axis=0)
    bottom = bottom - half_square * (first_flux + second_flux) * edge_rows[:, None, None]
    above = jnp.concatenate([zero_plane, above, zero_plane], axis=0)
    depth = lax.broadcasted_iota(jnp.int32, settled.shape, 3)
    fluid_field = settled + jnp.where(
        depth == 0, bottom[..., None], jnp.where(depth == 1, above[..., None], 0.0)
    )
    return (fluid_field, current)


def solution(mesh):
    return jax.shard_map(
        local,
        mesh=mesh,
        in_specs=(
            P(None, "sec", "blk", None),
            P("sec", "blk", None),
            P(),
            P(),
            P(None, "sec", "blk"),
            P(("sec", "blk"), None, None, None),
            P(("sec", "blk"), None),
            P(("sec", "blk"), None),
            P(("sec", "blk")),
            P(None, ("sec", "blk")),
            P(None, ("sec", "blk")),
            P(("sec", "blk"), None, None, None),
            P(("sec", "blk"), None),
        ),
        out_specs=(P(None, "sec", "blk", None), P(None, ("sec", "blk"))),
        check_vma=False,
    )
```
